256 devices in a mesh: orbit: 16 (over z, core), space: 16 (over x, y).
Axes of the slice: x: 4, y: 4, z: 8, core: 2. Of those that a mesh axis runs over, the one named last changes fastest.
Arguments:
- queries: bfloat16 [16, 32, 64, 2240], P('orbit', 'space'), may hold values from -6 to 6
- keys_in: bfloat16 [16, 32, 64, 2240], P('orbit', 'space'), may hold values from -6 to 6
- values: bfloat16 [16, 32, 64, 2240], P('orbit', 'space'), may hold values from -6 to 6
- conv_weight: bfloat16 [3, 3, 2240], replicated, may hold values from -2 to 2
- grad_out: bfloat16 [16, 32, 64, 2240], P('orbit', 'space'), may hold values from -6 to 6
Outputs:
- attended: bfloat16 [16, 32, 64, 2240], P('orbit', 'space')
- grad_query: bfloat16 [16, 32, 64, 2240], P('orbit', 'space')
- grad_key: bfloat16 [16, 32, 64, 2240], P('orbit', 'space')
- grad_value: bfloat16 [16, 32, 64, 2240], P('orbit', 'space')
The draws below stay inside these ranges and needn't reach their ends.
All inputs are finite; a program needn't handle non-finite values.
Results may differ from the reference program's by a relative error of at most 0.0079.
Values may be sent and summed in bfloat16 or wider, within the bound.
No kernel may reach another device: no remote copies, remote signals or barrier semaphores. Data moves between devices by JAX's collectives and lax.ppermute only.
A program may use at most 128 MiB of HBM per device.

```python
import math
import jax
import jax.numpy as jnp
from jax import lax

HEADS = 20
HD = 112
D = 2240
COLS = 64
LROWS = 32
VIEWS = 16


def offset_field(key, view_scale, row_scale):
    key_base, second, last_key = jax.random.split(key, 3)
    field_shape = (VIEWS, LROWS, COLS, D)
    base_field = jax.random.normal(key_base, field_shape, jnp.float32)
    view_offset = jax.random.normal(second, (VIEWS, 1, 1, D), jnp.float32) * view_scale
    row_offset = jax.random.normal(last_key, (VIEWS, LROWS, 1, D), jnp.float32) * row_scale
    return jnp.clip(base_field + view_offset + row_offset, -6.0, 6.0)


def draw_queries(key, part):
    key = jax.random.fold_in(key, 101)
    key_base, second = jax.random.split(key)
    field_shape = (VIEWS, LROWS, COLS, HEADS, HD)
    base_field = jax.random.normal(key_base, field_shape, jnp.float32)
    spread = jnp.exp(jax.random.uniform(second, (VIEWS, LROWS, COLS, HEADS, 1), jnp.float32, math.log(0.02), math.log(1.5)))
    return jnp.clip(base_field * spread, -6.0, 6.0).reshape(VIEWS, LROWS, COLS, D).astype(jnp.bfloat16)


def draw_keys_in(key, part):
    return offset_field(jax.random.fold_in(key, 202), 0.7, 0.4).astype(jnp.bfloat16)


def draw_values(key, part):
    return offset_field(jax.random.fold_in(key, 303), 1.0, 0.6).astype(jnp.bfloat16)


def draw_grad_out(key, part):
    return offset_field(jax.random.fold_in(key, 404), 0.8, 0.5).astype(jnp.bfloat16)


def centred(rng, shape, scale, bound, held_as=jnp.bfloat16):
    return jnp.clip(scale * jax.random.normal(rng, shape, jnp.float32), -bound, bound).astype(held_as)


def setup_inputs(seed: int = 0) -> dict:
    splits = jax.random.split(jax.random.key(seed), 6)
    return {
        "queries": draw_queries(jax.random.fold_in(splits[5], 71), 0),
        "keys_in": draw_keys_in(jax.random.fold_in(splits[5], 71), 0),
        "values": draw_values(jax.random.fold_in(splits[5], 71), 0),
        "conv_weight": centred(splits[3], (3, 3, D), 9 ** -0.5, 2.0),
        "grad_out": draw_grad_out(jax.random.fold_in(splits[5], 71), 0),
    }


def conv_apply(source_field, conv_weight):
    padded = jnp.pad(source_field.astype(jnp.float32), ((1, 1), (1, 1), (0, 0)))
    weight_wide = conv_weight.astype(jnp.float32)
    running_sum = jnp.zeros(source_field.shape, jnp.float32)
    for row_step in range(3):
        for col_step in range(3):
            running_sum = running_sum + weight_wide[row_step, col_step] * padded[row_step:row_step + LROWS, col_step:col_step + COLS]
    return running_sum


def conv_back(source_field, conv_weight):
    padded = jnp.pad(source_field.astype(jnp.float32), ((1, 1), (1, 1), (0, 0)))
    weight_wide = conv_weight.astype(jnp.float32)
    running_sum = jnp.zeros(source_field.shape, jnp.float32)
    for row_step in range(3):
        for col_step in range(3):
            running_sum = running_sum + weight_wide[row_step, col_step] * padded[2 - row_step:2 - row_step + LROWS, 2 - col_step:2 - col_step + COLS]
    return running_sum


def reference(queries, keys_in, values, conv_weight, grad_out):
    token_count = LROWS * COLS
    heads_shape = (token_count, HEADS, HD)
    counts = (jnp.arange(VIEWS, dtype=jnp.float32) + 1.0) * float(token_count)

    def local_state(pair_items):
        key_view, value_view = pair_items
        key_feat = jax.nn.relu(key_view).reshape(heads_shape).astype(jnp.float32)
        value_heads = value_view.reshape(heads_shape).astype(jnp.float32)
        state_part = jnp.einsum("thd,the->hde", key_feat, value_heads)
        norm_part = jnp.sum(key_feat, axis=0)
        return state_part, norm_part

    state_parts, norm_parts = lax.map(local_state, (keys_in, values))
    state_b = (jnp.cumsum(state_parts, 0) / counts[:, None, None, None]).astype(jnp.bfloat16)
    norm_b = (jnp.cumsum(norm_parts, 0) / counts[:, None, None]).astype(jnp.bfloat16)

    def forward_view(view_items):
        query_view, value_view, grad_view, state_view, norm_view = view_items
        query_feat = jax.nn.relu(query_view).reshape(heads_shape).astype(jnp.float32)
        state_wide = state_view.astype(jnp.float32)
        norm_wide = norm_view.astype(jnp.float32)
        numerator = jnp.einsum("thd,hde->the", query_feat, state_wide)
        denominator = jnp.einsum("thd,hd->th", query_feat, norm_wide) + 1.0
        attention = numerator / denominator[..., None]
        attended = (attention.reshape(LROWS, COLS, HEADS * HD) + conv_apply(value_view, conv_weight)).astype(jnp.bfloat16)
        grad_wide = grad_view.reshape(heads_shape).astype(jnp.float32)
        numerator_grad = (grad_wide / denominator[..., None]).astype(jnp.bfloat16).astype(jnp.float32)
        denominator_grad = (-jnp.sum(grad_wide * numerator, -1) / (denominator * denominator)).astype(jnp.bfloat16).astype(jnp.float32)
        query_grad = jnp.einsum("the,hde->thd", numerator_grad, state_wide) + denominator_grad[..., None] * norm_wide[None]
        grad_query = jnp.where(query_view.reshape(heads_shape) > 0, query_grad, 0.0).astype(jnp.bfloat16).reshape(LROWS, COLS, HEADS * HD)
        state_grad = jnp.einsum("thd,the->hde", query_feat, numerator_grad)
        norm_grad = jnp.einsum("thd,th->hd", query_feat, denominator_grad)
        return attended, grad_query, state_grad, norm_grad

    attended, grad_query, state_grads, norm_grads = lax.map(forward_view, (queries, values, grad_out, state_b, norm_b))
    scaled_state = state_grads / counts[:, None, None, None]
    scaled_norm = norm_grads / counts[:, None, None]
    back_state = jnp.flip(jnp.cumsum(jnp.flip(scaled_state, 0), 0), 0).astype(jnp.bfloat16)
    back_norm = jnp.flip(jnp.cumsum(jnp.flip(scaled_norm, 0), 0), 0).astype(jnp.bfloat16)

    def backward_view(view_items):
        key_view, value_view, grad_view, state_view, norm_view = view_items
        key_feat = jax.nn.relu(key_view).reshape(heads_shape).astype(jnp.float32)
        value_heads = value_view.reshape(heads_shape).astype(jnp.float32)
        state_wide = state_view.astype(jnp.float32)
        key_grad = jnp.einsum("the,hde->thd", value_heads, state_wide) + norm_view.astype(jnp.float32)[None]
        grad_key = jnp.where(key_view.reshape(heads_shape) > 0, key_grad, 0.0).astype(jnp.bfloat16).reshape(LROWS, COLS, HEADS * HD)
        value_grad = jnp.einsum("thd,hde->the", key_feat, state_wide).reshape(LROWS, COLS, HEADS * HD) + conv_back(grad_view, conv_weight)
        return grad_key, value_grad.astype(jnp.bfloat16)

    grad_key, grad_value = lax.map(backward_view, (keys_in, values, grad_out, back_state, back_norm))
    return (attended, grad_query, grad_key, grad_value)
```

```python
import jax
import jax.numpy as jnp
from jax import lax
from jax.sharding import PartitionSpec as P

HEADS = 20
HD = 112


def padded(cells, sides, width):
    for axis, dim in sides:
        count = lax.axis_size(axis)
        ends = count - 1
        head = lax.slice_in_dim(cells, 0, width, axis=dim)
        tail = lax.slice_in_dim(cells, cells.shape[dim] - width, cells.shape[dim], axis=dim)
        cells = jnp.concatenate(
            [
                lax.ppermute(tail, axis, [(i, (i + 1) % count) for i in range(ends)]),
                cells,
                lax.ppermute(head, axis, [((i + 1) % count, i) for i in range(ends)]),
            ],
            axis=dim,
        )
    return cells


def spread_states(state_part, norm_part, reverse, counts):
    space = lax.axis_size("space")
    orbit = lax.axis_size("orbit")
    place = lax.axis_index("orbit")
    flat = jnp.concatenate([state_part.reshape(-1), norm_part.reshape(-1)])
    total = flat.shape[0]
    chunk = -(-total // (space * 128)) * 128
    flat = jnp.pad(flat, (0, chunk * space - total))
    pieces = lax.all_to_all(flat.reshape(space, chunk), "space", 0, 0, tiled=True)
    whole = jnp.sum(pieces, axis=0)
    if not reverse:
        gathered = lax.all_gather(whole, "orbit")
        views = jnp.arange(orbit)
        keep = views <= place
        summed = jnp.sum(jnp.where(keep[:, None], gathered, 0.0), axis=0)
        summed = summed / counts
    else:
        whole = whole / counts
        gathered = lax.all_gather(whole, "orbit")
        views = jnp.arange(orbit)
        keep = views >= place
        summed = jnp.sum(jnp.where(keep[:, None], gathered, 0.0), axis=0)
    rounded = summed.astype(jnp.bfloat16)
    full = lax.all_gather(rounded, "space", tiled=True)[:total]
    size = state_part.size
    return full[:size].reshape(state_part.shape), full[size:].reshape(norm_part.shape)


def on_device(queries, keys_in, values, conv_weight, grad_out):
    view_count, row_count, col_count, feature_width = queries.shape
    token_count = row_count * col_count
    value_rows, grad_rows = (
        padded(values, (("space", 1),), 1),
        padded(grad_out, (("space", 1),), 1),
    )
    heads_shape = (token_count, HEADS, HD)
    query_feat = jax.nn.relu(queries).reshape(heads_shape)
    key_feat = jax.nn.relu(keys_in).reshape(heads_shape)
    value_heads = values.reshape(heads_shape)
    grad_heads = grad_out.reshape(heads_shape)
    place = lax.axis_index("orbit")
    count = (place.astype(jnp.float32) + 1.0) * float(
        row_count * lax.axis_size("space") * col_count
    )
    state_part = jnp.einsum(
        "thd,the->hde", key_feat, value_heads, preferred_element_type=jnp.float32
    )
    norm_part = jnp.sum(key_feat, axis=0, dtype=jnp.float32)
    state_b, norm_b = spread_states(state_part, norm_part, False, count)
    numerator = jnp.einsum(
        "thd,hde->the", query_feat, state_b, preferred_element_type=jnp.float32
    )
    denominator = (
        jnp.einsum("thd,hd->th", query_feat, norm_b, preferred_element_type=jnp.float32) + 1.0
    )
    weight_wide = conv_weight.astype(jnp.float32)
    value_pad = jnp.pad(value_rows, ((0, 0), (0, 0), (1, 1), (0, 0)))
    grad_pad = jnp.pad(grad_rows, ((0, 0), (0, 0), (1, 1), (0, 0)))
    conv_term = jnp.zeros(queries.shape, jnp.float32)
    conv_grad = jnp.zeros(queries.shape, jnp.float32)
    for row_step in range(3):
        for col_step in range(3):
            conv_term = conv_term + weight_wide[row_step, col_step] * value_pad[
                :, row_step : row_step + row_count, col_step : col_step + col_count
            ].astype(jnp.float32)
            conv_grad = conv_grad + weight_wide[row_step, col_step] * grad_pad[
                :, 2 - row_step : 2 - row_step + row_count, 2 - col_step : 2 - col_step + col_count
            ].astype(jnp.float32)
    attention = numerator / denominator[..., None]
    attended = (attention.reshape(queries.shape) + conv_term).astype(jnp.bfloat16)
    grad_wide = grad_heads.astype(jnp.float32)
    numerator_grad = (grad_wide / denominator[..., None]).astype(jnp.bfloat16)
    denominator_grad = (-jnp.sum(grad_wide * numerator, -1) / (denominator * denominator)).astype(
        jnp.bfloat16
    )
    query_grad = jnp.einsum(
        "the,hde->thd", numerator_grad, state_b, preferred_element_type=jnp.float32
    )
    query_grad = (
        query_grad
        + denominator_grad.astype(jnp.float32)[..., None] * norm_b.astype(jnp.float32)[None]
    )
    grad_query = (
        jnp.where(queries.reshape(heads_shape) > 0, query_grad, 0.0)
        .astype(jnp.bfloat16)
        .reshape(queries.shape)
    )
    state_grad = jnp.einsum(
        "thd,the->hde", query_feat, numerator_grad, preferred_element_type=jnp.float32
    )
    norm_grad = jnp.einsum(
        "thd,th->hd", query_feat, denominator_grad, preferred_element_type=jnp.float32
    )
    back_state, back_norm = spread_states(state_grad, norm_grad, True, count)
    key_grad = jnp.einsum(
        "the,hde->thd", value_heads, back_state, preferred_element_type=jnp.float32
    )
    key_grad = key_grad + back_norm.astype(jnp.float32)[None]
    grad_key = (
        jnp.where(keys_in.reshape(heads_shape) > 0, key_grad, 0.0)
        .astype(jnp.bfloat16)
        .reshape(queries.shape)
    )
    value_grad = (
        jnp.einsum(
            "thd,hde->the", key_feat, back_state, preferred_element_type=jnp.float32
        ).reshape(queries.shape)
        + conv_grad
    )
    grad_value = value_grad.astype(jnp.bfloat16)
    return (attended, grad_query, grad_key, grad_value)


def solution(mesh):
    placed = (
        P("orbit", "space", None, None),
        P("orbit", "space", None, None),
        P("orbit", "space", None, None),
        P(),
        P("orbit", "space", None, None),
    )
    return jax.shard_map(
        on_device,
        mesh=mesh,
        in_specs=placed,
        out_specs=(
            P("orbit", "space", None, None),
            P("orbit", "space", None, None),
            P("orbit", "space", None, None),
            P("orbit", "space", None, None),
        ),
        check_vma=False,
    )
```

```python
import jax
import jax.numpy as jnp
from jax import lax
from jax.experimental import pallas as pl
from jax.sharding import PartitionSpec as P

HEADS = 20
HD = 112


def padded_pair(cells, width):
    count = lax.axis_size("space")
    ends = count - 1
    rows = cells.shape[2]
    head = cells[:, :, :width]
    tail = cells[:, :, rows - width :]
    return jnp.concatenate(
        [
            lax.ppermute(tail, "space", [(i, (i + 1) % count) for i in range(ends)]),
            cells,
            lax.ppermute(head, "space", [((i + 1) % count, i) for i in range(ends)]),
        ],
        axis=2,
    )


def part_kernel(k_ref, v_ref, s_ref, n_ref):
    for h in range(HEADS):
        cols = slice(h * HD, (h + 1) * HD)
        kf = jnp.maximum(k_ref[:, cols], 0)
        vh = v_ref[:, cols]
        s_ref[h] = lax.dot_general(
            kf, vh, (((0,), (0,)), ((), ())), preferred_element_type=jnp.float32
        )
        n_ref[h : h + 1, :] = jnp.sum(kf.astype(jnp.float32), axis=0, keepdims=True)


def forward_kernel(q_ref, g_ref, c_ref, s_ref, n_ref, a_ref, gq_ref, sg_ref, ng_ref):
    for h in range(HEADS):
        cols = slice(h * HD, (h + 1) * HD)
        qh = q_ref[:, cols]
        qf = jnp.maximum(qh, 0)
        qw = qf.astype(jnp.float32)
        state = s_ref[h]
        norm = n_ref[h : h + 1, :].astype(jnp.float32)
        numerator = jnp.dot(qf, state, preferred_element_type=jnp.float32)
        denominator = jnp.sum(qw * norm, axis=1, keepdims=True) + 1.0
        a_ref[:, cols] = (numerator / denominator + c_ref[:, cols]).astype(jnp.bfloat16)
        gw = g_ref[:, cols].astype(jnp.float32)
        num_grad = (gw / denominator).astype(jnp.bfloat16)
        den_grad = (
            -jnp.sum(gw * numerator, axis=1, keepdims=True) / (denominator * denominator)
        ).astype(jnp.bfloat16).astype(jnp.float32)
        query_grad = lax.dot_general(
            num_grad, state, (((1,), (1,)), ((), ())), preferred_element_type=jnp.float32
        )
        query_grad = query_grad + den_grad * norm
        gq_ref[:, cols] = jnp.where(qh > 0, query_grad, 0.0).astype(jnp.bfloat16)
        sg_ref[h] = lax.dot_general(
            qf, num_grad, (((0,), (0,)), ((), ())), preferred_element_type=jnp.float32
        )
        ng_ref[h : h + 1, :] = jnp.sum(den_grad * qw, axis=0, keepdims=True)


def backward_kernel(k_ref, v_ref, c_ref, s_ref, n_ref, gk_ref, gv_ref):
    for h in range(HEADS):
        cols = slice(h * HD, (h + 1) * HD)
        kh = k_ref[:, cols]
        kf = jnp.maximum(kh, 0)
        vh = v_ref[:, cols]
        state = s_ref[h]
        norm = n_ref[h : h + 1, :].astype(jnp.float32)
        key_grad = lax.dot_general(
            vh, state, (((1,), (1,)), ((), ())), preferred_element_type=jnp.float32
        )
        gk_ref[:, cols] = jnp.where(kh > 0, key_grad + norm, 0.0).astype(jnp.bfloat16)
        value_grad = jnp.dot(kf, state, preferred_element_type=jnp.float32) + c_ref[:, cols]
        gv_ref[:, cols] = value_grad.astype(jnp.bfloat16)


def spread_states(state_part, norm_part, reverse, counts):
    space = lax.axis_size("space")
    orbit = lax.axis_size("orbit")
    place = lax.axis_index("orbit")
    flat = jnp.concatenate([state_part.reshape(-1), norm_part.reshape(-1)])
    total = flat.shape[0]
    chunk = -(-total // (space * 128)) * 128
    flat = jnp.pad(flat, (0, chunk * space - total))
    pieces = lax.all_to_all(flat.reshape(space, chunk), "space", 0, 0, tiled=True)
    whole = jnp.sum(pieces, axis=0)
    if not reverse:
        gathered = lax.all_gather(whole, "orbit")
        views = jnp.arange(orbit)
        keep = views <= place
        summed = jnp.sum(jnp.where(keep[:, None], gathered, 0.0), axis=0)
        summed = summed / counts
    else:
        whole = whole / counts
        gathered = lax.all_gather(whole, "orbit")
        views = jnp.arange(orbit)
        keep = views >= place
        summed = jnp.sum(jnp.where(keep[:, None], gathered, 0.0), axis=0)
    rounded = summed.astype(jnp.bfloat16)
    full = lax.all_gather(rounded, "space", tiled=True)[:total]
    size = state_part.size
    return full[:size].reshape(state_part.shape), full[size:].reshape(norm_part.shape)


def on_device(queries, keys_in, values, conv_weight, grad_out):
    view_count, row_count, col_count, feature_width = queries.shape
    token_count = view_count * row_count * col_count
    flat_shape = (token_count, feature_width)
    q2 = queries.reshape(flat_shape)
    k2 = keys_in.reshape(flat_shape)
    v2 = values.reshape(flat_shape)
    g2 = grad_out.reshape(flat_shape)
    place = lax.axis_index("orbit")
    count = (place.astype(jnp.float32) + 1.0) * float(
        row_count * lax.axis_size("space") * col_count
    )
    f32 = jnp.float32
    state_part, norm_part = pl.pallas_call(
        part_kernel,
        out_shape=(
            jax.ShapeDtypeStruct((HEADS, HD, HD), f32),
            jax.ShapeDtypeStruct((HEADS, HD), f32),
        ),
    )(k2, v2)
    state_b, norm_b = spread_states(state_part, norm_part, False, count)

    pair = padded_pair(jnp.stack([values, grad_out]), 1)
    pair = jnp.pad(pair, ((0, 0), (0, 0), (0, 0), (1, 1), (0, 0)))
    value_pad, grad_pad = pair[0], pair[1]
    weight_wide = conv_weight.astype(f32)
    conv_term = jnp.zeros(queries.shape, f32)
    conv_grad = jnp.zeros(queries.shape, f32)
    for row_step in range(3):
        for col_step in range(3):
            conv_term = conv_term + weight_wide[row_step, col_step] * value_pad[
                :, row_step : row_step + row_count, col_step : col_step + col_count
            ].astype(f32)
            conv_grad = conv_grad + weight_wide[row_step, col_step] * grad_pad[
                :, 2 - row_step : 2 - row_step + row_count, 2 - col_step : 2 - col_step + col_count
            ].astype(f32)

    bf = jnp.bfloat16
    attended, grad_query, state_grad, norm_grad = pl.pallas_call(
        forward_kernel,
        out_shape=(
            jax.ShapeDtypeStruct(flat_shape, bf),
            jax.ShapeDtypeStruct(flat_shape, bf),
            jax.ShapeDtypeStruct((HEADS, HD, HD), f32),
            jax.ShapeDtypeStruct((HEADS, HD), f32),
        ),
    )(q2, g2, conv_term.reshape(flat_shape), state_b, norm_b)
    back_state, back_norm = spread_states(state_grad, norm_grad, True, count)
    grad_key, grad_value = pl.pallas_call(
        backward_kernel,
        out_shape=(
            jax.ShapeDtypeStruct(flat_shape, bf),
            jax.ShapeDtypeStruct(flat_shape, bf),
        ),
    )(k2, v2, conv_grad.reshape(flat_shape), back_state, back_norm)
    shape = queries.shape
    return (
        attended.reshape(shape),
        grad_query.reshape(shape),
        grad_key.reshape(shape),
        grad_value.reshape(shape),
    )


def solution(mesh):
    placed = (
        P("orbit", "space", None, None),
        P("orbit", "space", None, None),
        P("orbit", "space", None, None),
        P(),
        P("orbit", "space", None, None),
    )
    return jax.shard_map(
        on_device,
        mesh=mesh,
        in_specs=placed,
        out_specs=(
            P("orbit", "space", None, None),
            P("orbit", "space", None, None),
            P("orbit", "space", None, None),
            P("orbit", "space", None, None),
        ),
        check_vma=False,
    )
```

```python
import jax
import jax.numpy as jnp
from jax import lax
from jax.experimental import pallas as pl
from jax.sharding import PartitionSpec as P

HEADS = 20
HD = 112


def padded_pair(cells, width):
    count = lax.axis_size("space")
    ends = count - 1
    rows = cells.shape[2]
    head = cells[:, :, :width]
    tail = cells[:, :, rows - width :]
    return jnp.concatenate(
        [
            lax.ppermute(tail, "space", [(i, (i + 1) % count) for i in range(ends)]),
            cells,
            lax.ppermute(head, "space", [((i + 1) % count, i) for i in range(ends)]),
        ],
        axis=2,
    )


ROWS = HEADS * HD
PACKED = 2304


def part_kernel(k_ref, v_ref, s_ref):
    s_ref[ROWS:, :] = jnp.zeros((PACKED - ROWS, HD), jnp.float32)
    for h in range(HEADS):
        cols = slice(h * HD, (h + 1) * HD)
        kf = jnp.maximum(k_ref[:, cols], 0)
        vh = v_ref[:, cols]
        s_ref[h * HD : (h + 1) * HD, :] = lax.dot_general(
            kf, vh, (((0,), (0,)), ((), ())), preferred_element_type=jnp.float32
        )
        s_ref[ROWS + h : ROWS + h + 1, :] = jnp.sum(
            kf.astype(jnp.float32), axis=0, keepdims=True
        )


def forward_kernel(q_ref, g_ref, c_ref, s_ref, a_ref, gq_ref, sg_ref):
    sg_ref[ROWS:, :] = jnp.zeros((PACKED - ROWS, HD), jnp.float32)
    for h in range(HEADS):
        cols = slice(h * HD, (h + 1) * HD)
        qh = q_ref[:, cols]
        qf = jnp.maximum(qh, 0)
        qw = qf.astype(jnp.float32)
        state = s_ref[h * HD : (h + 1) * HD, :]
        norm = s_ref[ROWS + h : ROWS + h + 1, :].astype(jnp.float32)
        numerator = jnp.dot(qf, state, preferred_element_type=jnp.float32)
        denominator = jnp.sum(qw * norm, axis=1, keepdims=True) + 1.0
        inverse = 1.0 / denominator
        a_ref[:, cols] = (numerator * inverse + c_ref[:, cols]).astype(jnp.bfloat16)
        gw = g_ref[:, cols].astype(jnp.float32)
        num_grad = (gw * inverse).astype(jnp.bfloat16)
        den_grad = (
            -jnp.sum(gw * numerator, axis=1, keepdims=True) * (inverse * inverse)
        ).astype(jnp.bfloat16).astype(jnp.float32)
        query_grad = lax.dot_general(
            num_grad, state, (((1,), (1,)), ((), ())), preferred_element_type=jnp.float32
        )
        query_grad = query_grad + den_grad * norm
        gq_ref[:, cols] = jnp.where(qh > 0, query_grad, 0.0).astype(jnp.bfloat16)
        sg_ref[h * HD : (h + 1) * HD, :] = lax.dot_general(
            qf, num_grad, (((0,), (0,)), ((), ())), preferred_element_type=jnp.float32
        )
        sg_ref[ROWS + h : ROWS + h + 1, :] = jnp.sum(den_grad * qw, axis=0, keepdims=True)


def backward_kernel(k_ref, v_ref, c_ref, s_ref, gk_ref, gv_ref):
    for h in range(HEADS):
        cols = slice(h * HD, (h + 1) * HD)
        kh = k_ref[:, cols]
        kf = jnp.maximum(kh, 0)
        vh = v_ref[:, cols]
        state = s_ref[h * HD : (h + 1) * HD, :]
        norm = s_ref[ROWS + h : ROWS + h + 1, :].astype(jnp.float32)
        key_grad = lax.dot_general(
            vh, state, (((1,), (1,)), ((), ())), preferred_element_type=jnp.float32
        )
        gk_ref[:, cols] = jnp.where(kh > 0, key_grad + norm, 0.0).astype(jnp.bfloat16)
        value_grad = jnp.dot(kf, state, preferred_element_type=jnp.float32) + c_ref[:, cols]
        gv_ref[:, cols] = value_grad.astype(jnp.bfloat16)


def spread_states(packed, reverse, counts):
    space = lax.axis_size("space")
    orbit = lax.axis_size("orbit")
    place = lax.axis_index("orbit")
    pieces = lax.all_to_all(packed.reshape(space, -1, HD), "space", 0, 0, tiled=True)
    whole = jnp.sum(pieces, axis=0)
    views = jnp.arange(orbit)
    if not reverse:
        gathered = lax.all_gather(whole, "orbit")
        keep = views <= place
        summed = jnp.sum(jnp.where(keep[:, None, None], gathered, 0.0), axis=0)
        summed = summed / counts
    else:
        whole = whole / counts
        gathered = lax.all_gather(whole, "orbit")
        keep = views >= place
        summed = jnp.sum(jnp.where(keep[:, None, None], gathered, 0.0), axis=0)
    rounded = summed.astype(jnp.bfloat16)
    return lax.all_gather(rounded, "space", tiled=True)


def on_device(queries, keys_in, values, conv_weight, grad_out):
    view_count, row_count, col_count, feature_width = queries.shape
    token_count = view_count * row_count * col_count
    flat_shape = (token_count, feature_width)
    q2 = queries.reshape(flat_shape)
    k2 = keys_in.reshape(flat_shape)
    v2 = values.reshape(flat_shape)
    g2 = grad_out.reshape(flat_shape)
    place = lax.axis_index("orbit")
    count = (place.astype(jnp.float32) + 1.0) * float(
        row_count * lax.axis_size("space") * col_count
    )
    f32 = jnp.float32
    packed_part = pl.pallas_call(
        part_kernel, out_shape=jax.ShapeDtypeStruct((PACKED, HD), f32)
    )(k2, v2)
    state_b = spread_states(packed_part, False, count)

    pair = padded_pair(jnp.stack([values, grad_out]), 1)
    pair = jnp.pad(pair, ((0, 0), (0, 0), (0, 0), (1, 1), (0, 0)))
    value_pad, grad_pad = pair[0], pair[1]
    weight_wide = conv_weight.astype(f32)
    conv_term = jnp.zeros(queries.shape, f32)
    conv_grad = jnp.zeros(queries.shape, f32)
    for row_step in range(3):
        for col_step in range(3):
            conv_term = conv_term + weight_wide[row_step, col_step] * value_pad[
                :, row_step : row_step + row_count, col_step : col_step + col_count
            ].astype(f32)
            conv_grad = conv_grad + weight_wide[row_step, col_step] * grad_pad[
                :, 2 - row_step : 2 - row_step + row_count, 2 - col_step : 2 - col_step + col_count
            ].astype(f32)

    bf = jnp.bfloat16
    attended, grad_query, state_grad = pl.pallas_call(
        forward_kernel,
        out_shape=(
            jax.ShapeDtypeStruct(flat_shape, bf),
            jax.ShapeDtypeStruct(flat_shape, bf),
            jax.ShapeDtypeStruct((PACKED, HD), f32),
        ),
    )(q2, g2, conv_term.reshape(flat_shape), state_b)
    back_state = spread_states(state_grad, True, count)
    grad_key, grad_value = pl.pallas_call(
        backward_kernel,
        out_shape=(
            jax.ShapeDtypeStruct(flat_shape, bf),
            jax.ShapeDtypeStruct(flat_shape, bf),
        ),
    )(k2, v2, conv_grad.reshape(flat_shape), back_state)
    shape = queries.shape
    return (
        attended.reshape(shape),
        grad_query.reshape(shape),
        grad_key.reshape(shape),
        grad_value.reshape(shape),
    )


def solution(mesh):
    placed = (
        P("orbit", "space", None, None),
        P("orbit", "space", None, None),
        P("orbit", "space", None, None),
        P(),
        P("orbit", "space", None, None),
    )
    return jax.shard_map(
        on_device,
        mesh=mesh,
        in_specs=placed,
        out_specs=(
            P("orbit", "space", None, None),
            P("orbit", "space", None, None),
            P("orbit", "space", None, None),
            P("orbit", "space", None, None),
        ),
        check_vma=False,
    )
```

```python
import jax
import jax.numpy as jnp
from jax import lax
from jax.experimental import pallas as pl
from jax.sharding import PartitionSpec as P

HEADS = 20
HD = 112


def padded_pair(cells, width):
    count = lax.axis_size("space")
    ends = count - 1
    rows = cells.shape[2]
    head = cells[:, :, :width]
    tail = cells[:, :, rows - width :]
    return jnp.concatenate(
        [
            lax.ppermute(tail, "space", [(i, (i + 1) % count) for i in range(ends)]),
            cells,
            lax.ppermute(head, "space", [((i + 1) % count, i) for i in range(ends)]),
        ],
        axis=2,
    )


ROWS = HEADS * HD
PACKED = 2304
LANES = 128
NORM = HD


def lane_one(tokens):
    lanes = lax.broadcasted_iota(jnp.int32, (tokens, LANES - HD), 1)
    return (lanes == 0).astype(jnp.bfloat16)


def part_kernel(k_ref, v_ref, s_ref):
    s_ref[ROWS:, :] = jnp.zeros((PACKED - ROWS, LANES), jnp.float32)
    extra = lane_one(k_ref.shape[0])
    for h in range(HEADS):
        cols = slice(h * HD, (h + 1) * HD)
        kf = jnp.maximum(k_ref[:, cols], 0)
        v_ext = jnp.concatenate([v_ref[:, cols], extra], axis=1)
        s_ref[h * HD : (h + 1) * HD, :] = lax.dot_general(
            kf, v_ext, (((0,), (0,)), ((), ())), preferred_element_type=jnp.float32
        )


def head_terms(qh, gh, state):
    qf = jnp.maximum(qh, 0)
    wide = jnp.dot(qf, state, preferred_element_type=jnp.float32)
    numerator = wide[:, :HD]
    denominator = wide[:, NORM : NORM + 1] + 1.0
    inverse = 1.0 / denominator
    gw = gh.astype(jnp.float32)
    num_grad = (gw * inverse).astype(jnp.bfloat16)
    den_grad = (
        -jnp.sum(gw * numerator, axis=1, keepdims=True) / (denominator * denominator)
    ).astype(jnp.bfloat16)
    pad = jnp.zeros((qh.shape[0], LANES - HD - 1), jnp.bfloat16)
    grads = jnp.concatenate([num_grad, den_grad, pad], axis=1)
    return qf, numerator, inverse, grads


def state_grad_kernel(q_ref, g_ref, s_ref, sg_ref):
    sg_ref[ROWS:, :] = jnp.zeros((PACKED - ROWS, LANES), jnp.float32)
    for h in range(HEADS):
        cols = slice(h * HD, (h + 1) * HD)
        state = s_ref[h * HD : (h + 1) * HD, :]
        qf, _, _, grads = head_terms(q_ref[:, cols], g_ref[:, cols], state)
        sg_ref[h * HD : (h + 1) * HD, :] = lax.dot_general(
            qf, grads, (((0,), (0,)), ((), ())), preferred_element_type=jnp.float32
        )


def forward_kernel(q_ref, g_ref, c_ref, s_ref, a_ref, gq_ref):
    for h in range(HEADS):
        cols = slice(h * HD, (h + 1) * HD)
        qh = q_ref[:, cols]
        state = s_ref[h * HD : (h + 1) * HD, :]
        _, numerator, inverse, grads = head_terms(qh, g_ref[:, cols], state)
        a_ref[:, cols] = (numerator * inverse + c_ref[:, cols]).astype(jnp.bfloat16)
        query_grad = lax.dot_general(
            grads, state, (((1,), (1,)), ((), ())), preferred_element_type=jnp.float32
        )
        gq_ref[:, cols] = jnp.where(qh > 0, query_grad, 0.0).astype(jnp.bfloat16)


def backward_kernel(k_ref, v_ref, c_ref, s_ref, gk_ref, gv_ref):
    extra = lane_one(k_ref.shape[0])
    for h in range(HEADS):
        cols = slice(h * HD, (h + 1) * HD)
        kh = k_ref[:, cols]
        kf = jnp.maximum(kh, 0)
        v_ext = jnp.concatenate([v_ref[:, cols], extra], axis=1)
        state = s_ref[h * HD : (h + 1) * HD, :]
        key_grad = lax.dot_general(
            v_ext, state, (((1,), (1,)), ((), ())), preferred_element_type=jnp.float32
        )
        gk_ref[:, cols] = jnp.where(kh > 0, key_grad, 0.0).astype(jnp.bfloat16)
        value_grad = jnp.dot(kf, state, preferred_element_type=jnp.float32)[:, :HD]
        gv_ref[:, cols] = (value_grad + c_ref[:, cols]).astype(jnp.bfloat16)


def spread_states(packed, reverse, counts):
    space = lax.axis_size("space")
    orbit = lax.axis_size("orbit")
    place = lax.axis_index("orbit")
    pieces = lax.all_to_all(packed.reshape(space, -1, LANES), "space", 0, 0, tiled=True)
    whole = jnp.sum(pieces, axis=0)
    views = jnp.arange(orbit)
    if not reverse:
        gathered = lax.all_gather(whole, "orbit")
        keep = views <= place
        summed = jnp.sum(jnp.where(keep[:, None, None], gathered, 0.0), axis=0)
        summed = summed / counts
    else:
        whole = whole / counts
        gathered = lax.all_gather(whole, "orbit")
        keep = views >= place
        summed = jnp.sum(jnp.where(keep[:, None, None], gathered, 0.0), axis=0)
    rounded = summed.astype(jnp.bfloat16)
    return lax.all_gather(rounded, "space", tiled=True)


def on_device(queries, keys_in, values, conv_weight, grad_out):
    view_count, row_count, col_count, feature_width = queries.shape
    token_count = view_count * row_count * col_count
    flat_shape = (token_count, feature_width)
    q2 = queries.reshape(flat_shape)
    k2 = keys_in.reshape(flat_shape)
    v2 = values.reshape(flat_shape)
    g2 = grad_out.reshape(flat_shape)
    place = lax.axis_index("orbit")
    count = (place.astype(jnp.float32) + 1.0) * float(
        row_count * lax.axis_size("space") * col_count
    )
    f32 = jnp.float32
    packed_part = pl.pallas_call(
        part_kernel, out_shape=jax.ShapeDtypeStruct((PACKED, LANES), f32)
    )(k2, v2)
    state_b = spread_states(packed_part, False, count)

    pair = padded_pair(jnp.stack([values, grad_out]), 1)
    pair = jnp.pad(pair, ((0, 0), (0, 0), (0, 0), (1, 1), (0, 0)))
    value_pad, grad_pad = pair[0], pair[1]
    weight_wide = conv_weight.astype(f32)
    conv_term = jnp.zeros(queries.shape, f32)
    conv_grad = jnp.zeros(queries.shape, f32)
    for row_step in range(3):
        for col_step in range(3):
            conv_term = conv_term + weight_wide[row_step, col_step] * value_pad[
                :, row_step : row_step + row_count, col_step : col_step + col_count
            ].astype(f32)
            conv_grad = conv_grad + weight_wide[row_step, col_step] * grad_pad[
                :, 2 - row_step : 2 - row_step + row_count, 2 - col_step : 2 - col_step + col_count
            ].astype(f32)

    bf = jnp.bfloat16
    state_grad = pl.pallas_call(
        state_grad_kernel, out_shape=jax.ShapeDtypeStruct((PACKED, LANES), f32)
    )(q2, g2, state_b)
    attended, grad_query = pl.pallas_call(
        forward_kernel,
        out_shape=(
            jax.ShapeDtypeStruct(flat_shape, bf),
            jax.ShapeDtypeStruct(flat_shape, bf),
        ),
    )(q2, g2, conv_term.reshape(flat_shape), state_b)
    back_state = spread_states(state_grad, True, count)
    grad_key, grad_value = pl.pallas_call(
        backward_kernel,
        out_shape=(
            jax.ShapeDtypeStruct(flat_shape, bf),
            jax.ShapeDtypeStruct(flat_shape, bf),
        ),
    )(k2, v2, conv_grad.reshape(flat_shape), back_state)
    shape = queries.shape
    return (
        attended.reshape(shape),
        grad_query.reshape(shape),
        grad_key.reshape(shape),
        grad_value.reshape(shape),
    )


def solution(mesh):
    placed = (
        P("orbit", "space", None, None),
        P("orbit", "space", None, None),
        P("orbit", "space", None, None),
        P(),
        P("orbit", "space", None, None),
    )
    return jax.shard_map(
        on_device,
        mesh=mesh,
        in_specs=placed,
        out_specs=(
            P("orbit", "space", None, None),
            P("orbit", "space", None, None),
            P("orbit", "space", None, None),
            P("orbit", "space", None, None),
        ),
        check_vma=False,
    )
```

```python
import jax
import jax.numpy as jnp
from jax import lax
from jax.experimental import pallas as pl
from jax.sharding import PartitionSpec as P

HEADS = 20
HD = 112


def padded_pair(cells, width):
    count = lax.axis_size("space")
    ends = count - 1
    rows = cells.shape[2]
    head = cells[:, :, :width]
    tail = cells[:, :, rows - width :]
    return jnp.concatenate(
        [
            lax.ppermute(tail, "space", [(i, (i + 1) % count) for i in range(ends)]),
            cells,
            lax.ppermute(head, "space", [((i + 1) % count, i) for i in range(ends)]),
        ],
        axis=2,
    )


ROWS = HEADS * HD
PACKED = 2304
LANES = 128
NORM = HD


def lane_one(tokens):
    lanes = lax.broadcasted_iota(jnp.int32, (tokens, LANES - HD), 1)
    return (lanes == 0).astype(jnp.bfloat16)


def part_kernel(k_ref, v_ref, s_ref):
    s_ref[ROWS:, :] = jnp.zeros((PACKED - ROWS, LANES), jnp.float32)
    extra = lane_one(k_ref.shape[0])
    for h in range(HEADS):
        cols = slice(h * HD, (h + 1) * HD)
        kf = jnp.maximum(k_ref[:, cols], 0)
        v_ext = jnp.concatenate([v_ref[:, cols], extra], axis=1)
        s_ref[h * HD : (h + 1) * HD, :] = lax.dot_general(
            kf, v_ext, (((0,), (0,)), ((), ())), preferred_element_type=jnp.float32
        )


def head_terms(qh, gh, state):
    qf = jnp.maximum(qh, 0)
    wide = jnp.dot(qf, state, preferred_element_type=jnp.float32)
    numerator = wide[:, :HD]
    denominator = wide[:, NORM : NORM + 1] + 1.0
    inverse = 1.0 / denominator
    gw = gh.astype(jnp.float32)
    num_grad = (gw * inverse).astype(jnp.bfloat16)
    den_grad = (
        -jnp.sum(gw * numerator, axis=1, keepdims=True) / (denominator * denominator)
    ).astype(jnp.bfloat16)
    pad = jnp.zeros((qh.shape[0], LANES - HD - 1), jnp.bfloat16)
    grads = jnp.concatenate([num_grad, den_grad, pad], axis=1)
    return qf, numerator, inverse, grads


def state_grad_kernel(q_ref, g_ref, s_ref, sg_ref):
    sg_ref[ROWS:, :] = jnp.zeros((PACKED - ROWS, LANES), jnp.float32)
    for h in range(HEADS):
        cols = slice(h * HD, (h + 1) * HD)
        state = s_ref[h * HD : (h + 1) * HD, :]
        qf, _, _, grads = head_terms(q_ref[:, cols], g_ref[:, cols], state)
        sg_ref[h * HD : (h + 1) * HD, :] = lax.dot_general(
            qf, grads, (((0,), (0,)), ((), ())), preferred_element_type=jnp.float32
        )


def forward_kernel(q_ref, g_ref, c_ref, s_ref, a_ref, gq_ref):
    for h in range(HEADS):
        cols = slice(h * HD, (h + 1) * HD)
        qh = q_ref[:, cols]
        state = s_ref[h * HD : (h + 1) * HD, :]
        _, numerator, inverse, grads = head_terms(qh, g_ref[:, cols], state)
        a_ref[:, cols] = (numerator * inverse + c_ref[:, cols]).astype(jnp.bfloat16)
        query_grad = lax.dot_general(
            grads, state, (((1,), (1,)), ((), ())), preferred_element_type=jnp.float32
        )
        gq_ref[:, cols] = jnp.where(qh > 0, query_grad, 0.0).astype(jnp.bfloat16)


def backward_kernel(k_ref, v_ref, c_ref, s_ref, gk_ref, gv_ref):
    extra = lane_one(k_ref.shape[0])
    for h in range(HEADS):
        cols = slice(h * HD, (h + 1) * HD)
        kh = k_ref[:, cols]
        kf = jnp.maximum(kh, 0)
        v_ext = jnp.concatenate([v_ref[:, cols], extra], axis=1)
        state = s_ref[h * HD : (h + 1) * HD, :]
        key_grad = lax.dot_general(
            v_ext, state, (((1,), (1,)), ((), ())), preferred_element_type=jnp.float32
        )
        gk_ref[:, cols] = jnp.where(kh > 0, key_grad, 0.0).astype(jnp.bfloat16)
        value_grad = jnp.dot(kf, state, preferred_element_type=jnp.float32)[:, :HD]
        gv_ref[:, cols] = (value_grad + c_ref[:, cols]).astype(jnp.bfloat16)


def spread_states(packed, reverse, counts):
    space = lax.axis_size("space")
    orbit = lax.axis_size("orbit")
    place = lax.axis_index("orbit")
    pieces = lax.all_to_all(packed.reshape(space, -1, LANES), "space", 0, 0, tiled=True)
    whole = jnp.sum(pieces, axis=0)[:, : NORM + 1]
    views = jnp.arange(orbit)
    if not reverse:
        gathered = lax.all_gather(whole, "orbit")
        keep = views <= place
        summed = jnp.sum(jnp.where(keep[:, None, None], gathered, 0.0), axis=0)
        summed = summed / counts
    else:
        whole = whole / counts
        gathered = lax.all_gather(whole, "orbit")
        keep = views >= place
        summed = jnp.sum(jnp.where(keep[:, None, None], gathered, 0.0), axis=0)
    rounded = jnp.pad(summed.astype(jnp.bfloat16), ((0, 0), (0, LANES - NORM - 1)))
    return lax.all_gather(rounded, "space", tiled=True)


def on_device_body(queries, keys_in, values, conv_weight, grad_out):
    view_count, row_count, col_count, feature_width = queries.shape
    token_count = view_count * row_count * col_count
    flat_shape = (token_count, feature_width)
    q2 = queries.reshape(flat_shape)
    k2 = keys_in.reshape(flat_shape)
    v2 = values.reshape(flat_shape)
    g2 = grad_out.reshape(flat_shape)
    place = lax.axis_index("orbit")
    count = (place.astype(jnp.float32) + 1.0) * float(
        row_count * lax.axis_size("space") * col_count
    )
    f32 = jnp.float32
    packed_part = pl.pallas_call(
        part_kernel, out_shape=jax.ShapeDtypeStruct((PACKED, LANES), f32)
    )(k2, v2)
    state_b = spread_states(packed_part, False, count)

    pair = padded_pair(jnp.stack([values, grad_out]), 1)
    pair = jnp.pad(pair, ((0, 0), (0, 0), (0, 0), (1, 1), (0, 0)))
    value_pad, grad_pad = pair[0], pair[1]
    weight_wide = conv_weight.astype(f32)
    conv_term = jnp.zeros(queries.shape, f32)
    conv_grad = jnp.zeros(queries.shape, f32)
    for row_step in range(3):
        for col_step in range(3):
            conv_term = conv_term + weight_wide[row_step, col_step] * value_pad[
                :, row_step : row_step + row_count, col_step : col_step + col_count
            ].astype(f32)
            conv_grad = conv_grad + weight_wide[row_step, col_step] * grad_pad[
                :, 2 - row_step : 2 - row_step + row_count, 2 - col_step : 2 - col_step + col_count
            ].astype(f32)

    bf = jnp.bfloat16
    state_grad = pl.pallas_call(
        state_grad_kernel, out_shape=jax.ShapeDtypeStruct((PACKED, LANES), f32)
    )(q2, g2, state_b)
    conv_flat = conv_term.reshape(flat_shape)
    attended, grad_query = pl.pallas_call(
        forward_kernel,
        out_shape=(
            jax.ShapeDtypeStruct(flat_shape, bf),
            jax.ShapeDtypeStruct(flat_shape, bf),
        ),
    )(q2, g2, conv_flat, state_b)
    back_state = spread_states(state_grad, True, count)
    grad_key, grad_value = pl.pallas_call(
        backward_kernel,
        out_shape=(
            jax.ShapeDtypeStruct(flat_shape, bf),
            jax.ShapeDtypeStruct(flat_shape, bf),
        ),
    )(k2, v2, conv_grad.reshape(flat_shape), back_state)
    shape = queries.shape
    return (
        attended.reshape(shape),
        grad_query.reshape(shape),
        grad_key.reshape(shape),
        grad_value.reshape(shape),
    )


def solution(mesh):
    placed = (
        P("orbit", "space", None, None),
        P("orbit", "space", None, None),
        P("orbit", "space", None, None),
        P(),
        P("orbit", "space", None, None),
    )
    return jax.shard_map(
        on_device_body,
        mesh=mesh,
        in_specs=placed,
        out_specs=(
            P("orbit", "space", None, None),
            P("orbit", "space", None, None),
            P("orbit", "space", None, None),
            P("orbit", "space", None, None),
        ),
        check_vma=False,
    )
```

```python
import jax
import jax.numpy as jnp
from jax import lax
from jax.experimental import pallas as pl
from jax.sharding import PartitionSpec as P

HEADS = 20
HD = 112


def padded_pair(cells, width):
    count = lax.axis_size("space")
    ends = count - 1
    rows = cells.shape[2]
    head = cells[:, :, :width]
    tail = cells[:, :, rows - width :]
    above = lax.ppermute(tail, "space", [(i, (i + 1) % count) for i in range(ends)])
    below = lax.ppermute(head, "space", [((i + 1) % count, i) for i in range(ends)])
    return jnp.concatenate([above, cells, below], axis=2)


ROWS = HEADS * HD
PACKED = 2304
LANES = 128
NORM = HD


def lane_one(tokens):
    lanes = lax.broadcasted_iota(jnp.int32, (tokens, LANES - HD), 1)
    return (lanes == 0).astype(jnp.bfloat16)


def part_kernel(k_ref, v_ref, s_ref):
    s_ref[ROWS:, :] = jnp.zeros((PACKED - ROWS, LANES), jnp.float32)
    extra = lane_one(k_ref.shape[0])
    for h in range(HEADS):
        cols = slice(h * HD, (h + 1) * HD)
        kf = jnp.maximum(k_ref[:, cols], 0)
        v_ext = jnp.concatenate([v_ref[:, cols], extra], axis=1)
        s_ref[h * HD : (h + 1) * HD, :] = lax.dot_general(
            kf, v_ext, (((0,), (0,)), ((), ())), preferred_element_type=jnp.float32
        )


def head_terms(qh, gh, state):
    qf = jnp.maximum(qh, 0)
    wide = jnp.dot(qf, state, preferred_element_type=jnp.float32)
    numerator = wide[:, :HD]
    denominator = wide[:, NORM : NORM + 1] + 1.0
    inverse = 1.0 / denominator
    gw = gh.astype(jnp.float32)
    num_grad = (gw * inverse).astype(jnp.bfloat16)
    den_grad = (
        -jnp.sum(gw * numerator, axis=1, keepdims=True) / (denominator * denominator)
    ).astype(jnp.bfloat16)
    pad = jnp.zeros((qh.shape[0], LANES - HD - 1), jnp.bfloat16)
    grads = jnp.concatenate([num_grad, den_grad, pad], axis=1)
    return qf, numerator, inverse, grads


def state_grad_kernel(q_ref, g_ref, s_ref, sg_ref):
    sg_ref[ROWS:, :] = jnp.zeros((PACKED - ROWS, LANES), jnp.float32)
    for h in range(HEADS):
        cols = slice(h * HD, (h + 1) * HD)
        state = s_ref[h * HD : (h + 1) * HD, :]
        qf, _, _, grads = head_terms(q_ref[:, cols], g_ref[:, cols], state)
        sg_ref[h * HD : (h + 1) * HD, :] = lax.dot_general(
            qf, grads, (((0,), (0,)), ((), ())), preferred_element_type=jnp.float32
        )


def forward_kernel(q_ref, g_ref, c_ref, s_ref, a_ref, gq_ref):
    for h in range(HEADS):
        cols = slice(h * HD, (h + 1) * HD)
        qh = q_ref[:, cols]
        state = s_ref[h * HD : (h + 1) * HD, :]
        _, numerator, inverse, grads = head_terms(qh, g_ref[:, cols], state)
        a_ref[:, cols] = (numerator * inverse + c_ref[:, cols]).astype(jnp.bfloat16)
        query_grad = lax.dot_general(
            grads, state, (((1,), (1,)), ((), ())), preferred_element_type=jnp.float32
        )
        gq_ref[:, cols] = jnp.where(qh > 0, query_grad, 0.0).astype(jnp.bfloat16)


def backward_kernel(k_ref, v_ref, c_ref, s_ref, gk_ref, gv_ref):
    extra = lane_one(k_ref.shape[0])
    for h in range(HEADS):
        cols = slice(h * HD, (h + 1) * HD)
        kh = k_ref[:, cols]
        kf = jnp.maximum(kh, 0)
        v_ext = jnp.concatenate([v_ref[:, cols], extra], axis=1)
        state = s_ref[h * HD : (h + 1) * HD, :]
        key_grad = lax.dot_general(
            v_ext, state, (((1,), (1,)), ((), ())), preferred_element_type=jnp.float32
        )
        gk_ref[:, cols] = jnp.where(kh > 0, key_grad, 0.0).astype(jnp.bfloat16)
        value_grad = jnp.dot(kf, state, preferred_element_type=jnp.float32)[:, :HD]
        gv_ref[:, cols] = (value_grad + c_ref[:, cols]).astype(jnp.bfloat16)


def spread_states(packed, reverse, counts):
    space = lax.axis_size("space")
    orbit = lax.axis_size("orbit")
    place = lax.axis_index("orbit")
    pieces = lax.all_to_all(packed.reshape(space, -1, LANES), "space", 0, 0, tiled=True)
    whole = jnp.sum(pieces, axis=0)[:, : NORM + 1]
    views = jnp.arange(orbit)
    if not reverse:
        gathered = lax.all_gather(whole, "orbit")
        keep = views <= place
        summed = jnp.sum(jnp.where(keep[:, None, None], gathered, 0.0), axis=0)
        summed = summed / counts
    else:
        whole = whole / counts
        gathered = lax.all_gather(whole, "orbit")
        keep = views >= place
        summed = jnp.sum(jnp.where(keep[:, None, None], gathered, 0.0), axis=0)
    rounded = jnp.pad(summed.astype(jnp.bfloat16), ((0, 0), (0, LANES - NORM - 1)))
    return lax.all_gather(rounded, "space", tiled=True)


def on_device_body(queries, keys_in, values, conv_weight, grad_out):
    view_count, row_count, col_count, feature_width = queries.shape
    token_count = view_count * row_count * col_count
    flat_shape = (token_count, feature_width)
    q2 = queries.reshape(flat_shape)
    k2 = keys_in.reshape(flat_shape)
    v2 = values.reshape(flat_shape)
    g2 = grad_out.reshape(flat_shape)
    place = lax.axis_index("orbit")
    count = (place.astype(jnp.float32) + 1.0) * float(
        row_count * lax.axis_size("space") * col_count
    )
    f32 = jnp.float32
    packed_part = pl.pallas_call(
        part_kernel, out_shape=jax.ShapeDtypeStruct((PACKED, LANES), f32)
    )(k2, v2)
    state_b = spread_states(packed_part, False, count)

    pair = padded_pair(jnp.stack([values, grad_out]), 1)
    pair = jnp.pad(pair, ((0, 0), (0, 0), (0, 0), (1, 1), (0, 0)))
    value_pad, grad_pad = pair[0], pair[1]
    weight_wide = conv_weight.astype(f32)
    conv_term = jnp.zeros(queries.shape, f32)
    conv_grad = jnp.zeros(queries.shape, f32)
    for row_step in range(3):
        for col_step in range(3):
            conv_term = conv_term + weight_wide[row_step, col_step] * value_pad[
                :, row_step : row_step + row_count, col_step : col_step + col_count
            ].astype(f32)
            conv_grad = conv_grad + weight_wide[row_step, col_step] * grad_pad[
                :, 2 - row_step : 2 - row_step + row_count, 2 - col_step : 2 - col_step + col_count
            ].astype(f32)

    bf = jnp.bfloat16
    state_grad = pl.pallas_call(
        state_grad_kernel, out_shape=jax.ShapeDtypeStruct((PACKED, LANES), f32)
    )(q2, g2, state_b)
    conv_flat = conv_term.reshape(flat_shape)
    attended, grad_query = pl.pallas_call(
        forward_kernel,
        out_shape=(
            jax.ShapeDtypeStruct(flat_shape, bf),
            jax.ShapeDtypeStruct(flat_shape, bf),
        ),
    )(q2, g2, conv_flat, state_b)
    back_state = spread_states(state_grad, True, count)
    grad_key, grad_value = pl.pallas_call(
        backward_kernel,
        out_shape=(
            jax.ShapeDtypeStruct(flat_shape, bf),
            jax.ShapeDtypeStruct(flat_shape, bf),
        ),
    )(k2, v2, conv_grad.reshape(flat_shape), back_state)
    shape = queries.shape
    return (
        attended.reshape(shape),
        grad_query.reshape(shape),
        grad_key.reshape(shape),
        grad_value.reshape(shape),
    )


def solution(mesh):
    placed = (
        P("orbit", "space", None, None),
        P("orbit", "space", None, None),
        P("orbit", "space", None, None),
        P(),
        P("orbit", "space", None, None),
    )
    return jax.shard_map(
        on_device_body,
        mesh=mesh,
        in_specs=placed,
        out_specs=(
            P("orbit", "space", None, None),
            P("orbit", "space", None, None),
            P("orbit", "space", None, None),
            P("orbit", "space", None, None),
        ),
        check_vma=False,
    )
```

```python
import jax
import jax.numpy as jnp
from jax import lax
from jax.experimental import pallas as pl
from jax.sharding import PartitionSpec as P

HEADS = 20
HD = 112


def padded_pair(cells, width):
    count = lax.axis_size("space")
    ends = count - 1
    rows = cells.shape[2]
    head = cells[:, :, :width]
    tail = cells[:, :, rows - width :]
    above = lax.ppermute(tail, "space", [(i, (i + 1) % count) for i in range(ends)])
    below = lax.ppermute(head, "space", [((i + 1) % count, i) for i in range(ends)])
    return jnp.concatenate([above, cells, below], axis=2)


ROWS = HEADS * HD
PACKED = 2304
LANES = 128
NORM = HD


def lane_one(tokens):
    lanes = lax.broadcasted_iota(jnp.int32, (tokens, LANES - HD), 1)
    return (lanes == 0).astype(jnp.bfloat16)


def part_kernel(k_ref, v_ref, s_ref):
    s_ref[ROWS:, :] = jnp.zeros((PACKED - ROWS, LANES), jnp.float32)
    extra = lane_one(k_ref.shape[0])
    for h in range(HEADS):
        cols = slice(h * HD, (h + 1) * HD)
        kf = jnp.maximum(k_ref[:, cols], 0)
        v_ext = jnp.concatenate([v_ref[:, cols], extra], axis=1)
        s_ref[h * HD : (h + 1) * HD, :] = lax.dot_general(
            kf, v_ext, (((0,), (0,)), ((), ())), preferred_element_type=jnp.float32
        )


def head_terms(qh, gh, state):
    qf = jnp.maximum(qh, 0)
    wide = jnp.dot(qf, state, preferred_element_type=jnp.float32)
    numerator = wide[:, :HD]
    denominator = wide[:, NORM : NORM + 1] + 1.0
    inverse = 1.0 / denominator
    gw = gh.astype(jnp.float32)
    num_grad = (gw * inverse).astype(jnp.bfloat16)
    den_grad = (
        -jnp.sum(gw * numerator, axis=1, keepdims=True) / (denominator * denominator)
    ).astype(jnp.bfloat16)
    pad = jnp.zeros((qh.shape[0], LANES - HD - 1), jnp.bfloat16)
    grads = jnp.concatenate([num_grad, den_grad, pad], axis=1)
    return qf, numerator, inverse, grads


def tile_kernel(q_ref, g_ref, k_ref, v_ref, qt_ref, qx_ref, gt_ref, kt_ref, vt_ref):
    tokens = q_ref.shape[0]
    zero = jnp.zeros((tokens, LANES - HD), jnp.bfloat16)
    extra = lane_one(tokens)
    for h in range(HEADS):
        cols = slice(h * HD, (h + 1) * HD)
        qf = jnp.concatenate([jnp.maximum(q_ref[:, cols], 0), zero], axis=1)
        qt_ref[h] = qf
        qx_ref[h] = qf.T
        gt_ref[h] = jnp.concatenate([g_ref[:, cols], zero], axis=1)
        kt_ref[h] = jnp.concatenate([jnp.maximum(k_ref[:, cols], 0), zero], axis=1)
        vt_ref[h] = jnp.concatenate([v_ref[:, cols], extra], axis=1)


def state_grad_kernel(qt_ref, qx_ref, gt_ref, s_ref, sg_ref):
    sg_ref[ROWS:, :] = jnp.zeros((PACKED - ROWS, LANES), jnp.float32)
    lanes = lax.broadcasted_iota(jnp.int32, (qt_ref.shape[1], LANES), 1)
    for h in range(HEADS):
        state = s_ref[h * HD : h * HD + LANES, :]
        wide = jnp.dot(qt_ref[h], state, preferred_element_type=jnp.float32)
        denominator = wide[:, NORM : NORM + 1] + 1.0
        inverse = 1.0 / denominator
        gw = gt_ref[h].astype(jnp.float32)
        num_grad = (gw * inverse).astype(jnp.bfloat16)
        den_grad = (
            -jnp.sum(gw * wide, axis=1, keepdims=True) / (denominator * denominator)
        ).astype(jnp.bfloat16)
        grads = jnp.where(lanes == NORM, den_grad, num_grad)
        sg = jnp.dot(qx_ref[h], grads, preferred_element_type=jnp.float32)
        sg_ref[h * HD : (h + 1) * HD, :] = sg[:HD]


def forward_kernel(q_ref, g_ref, c_ref, s_ref, a_ref, gq_ref):
    for h in range(HEADS):
        cols = slice(h * HD, (h + 1) * HD)
        qh = q_ref[:, cols]
        state = s_ref[h * HD : (h + 1) * HD, :]
        _, numerator, inverse, grads = head_terms(qh, g_ref[:, cols], state)
        a_ref[:, cols] = (numerator * inverse + c_ref[:, cols]).astype(jnp.bfloat16)
        query_grad = lax.dot_general(
            grads, state, (((1,), (1,)), ((), ())), preferred_element_type=jnp.float32
        )
        gq_ref[:, cols] = jnp.where(qh > 0, query_grad, 0.0).astype(jnp.bfloat16)


def backward_kernel(kt_ref, vt_ref, c_ref, s_ref, gk_ref, gv_ref):
    for h in range(HEADS):
        cols = slice(h * HD, (h + 1) * HD)
        kf = kt_ref[h]
        key_grad = lax.dot_general(
            vt_ref[h], s_ref[h * HD : (h + 1) * HD, :], (((1,), (1,)), ((), ())),
            preferred_element_type=jnp.float32,
        )
        gk_ref[:, cols] = jnp.where(kf[:, :HD] > 0, key_grad, 0.0).astype(jnp.bfloat16)
        state = s_ref[h * HD : h * HD + LANES, :]
        value_grad = jnp.dot(kf, state, preferred_element_type=jnp.float32)[:, :HD]
        gv_ref[:, cols] = (value_grad + c_ref[:, cols]).astype(jnp.bfloat16)


def spread_states(packed, reverse, counts):
    space = lax.axis_size("space")
    orbit = lax.axis_size("orbit")
    place = lax.axis_index("orbit")
    pieces = lax.all_to_all(packed.reshape(space, -1, LANES), "space", 0, 0, tiled=True)
    whole = jnp.sum(pieces, axis=0)[:, : NORM + 1]
    views = jnp.arange(orbit)
    if not reverse:
        gathered = lax.all_gather(whole, "orbit")
        keep = views <= place
        summed = jnp.sum(jnp.where(keep[:, None, None], gathered, 0.0), axis=0)
        summed = summed / counts
    else:
        whole = whole / counts
        gathered = lax.all_gather(whole, "orbit")
        keep = views >= place
        summed = jnp.sum(jnp.where(keep[:, None, None], gathered, 0.0), axis=0)
    rounded = jnp.pad(summed.astype(jnp.bfloat16), ((0, 0), (0, LANES - NORM - 1)))
    return lax.all_gather(rounded, "space", tiled=True)


def on_device_body(queries, keys_in, values, conv_weight, grad_out):
    view_count, row_count, col_count, feature_width = queries.shape
    token_count = view_count * row_count * col_count
    flat_shape = (token_count, feature_width)
    q2 = queries.reshape(flat_shape)
    k2 = keys_in.reshape(flat_shape)
    v2 = values.reshape(flat_shape)
    g2 = grad_out.reshape(flat_shape)
    place = lax.axis_index("orbit")
    count = (place.astype(jnp.float32) + 1.0) * float(
        row_count * lax.axis_size("space") * col_count
    )
    f32 = jnp.float32
    packed_part = pl.pallas_call(
        part_kernel, out_shape=jax.ShapeDtypeStruct((PACKED, LANES), f32)
    )(k2, v2)
    tile = jax.ShapeDtypeStruct((HEADS, token_count, LANES), jnp.bfloat16)
    q_tiles, q_cross, g_tiles, k_tiles, v_tiles = pl.pallas_call(
        tile_kernel, out_shape=(tile,) * 5
    )(q2, g2, k2, v2)
    state_b = spread_states(packed_part, False, count)

    pair = padded_pair(jnp.stack([values, grad_out]), 1)
    pair = jnp.pad(pair, ((0, 0), (0, 0), (0, 0), (1, 1), (0, 0)))
    value_pad, grad_pad = pair[0], pair[1]
    weight_wide = conv_weight.astype(f32)
    conv_term = jnp.zeros(queries.shape, f32)
    conv_grad = jnp.zeros(queries.shape, f32)
    for row_step in range(3):
        for col_step in range(3):
            conv_term = conv_term + weight_wide[row_step, col_step] * value_pad[
                :, row_step : row_step + row_count, col_step : col_step + col_count
            ].astype(f32)
            conv_grad = conv_grad + weight_wide[row_step, col_step] * grad_pad[
                :, 2 - row_step : 2 - row_step + row_count, 2 - col_step : 2 - col_step + col_count
            ].astype(f32)

    bf = jnp.bfloat16
    state_grad = pl.pallas_call(
        state_grad_kernel, out_shape=jax.ShapeDtypeStruct((PACKED, LANES), f32)
    )(q_tiles, q_cross, g_tiles, state_b)
    conv_flat = conv_term.reshape(flat_shape)
    attended, grad_query = pl.pallas_call(
        forward_kernel,
        out_shape=(
            jax.ShapeDtypeStruct(flat_shape, bf),
            jax.ShapeDtypeStruct(flat_shape, bf),
        ),
    )(q2, g2, conv_flat, state_b)
    back_state = spread_states(state_grad, True, count)
    grad_key, grad_value = pl.pallas_call(
        backward_kernel,
        out_shape=(
            jax.ShapeDtypeStruct(flat_shape, bf),
            jax.ShapeDtypeStruct(flat_shape, bf),
        ),
    )(k_tiles, v_tiles, conv_grad.reshape(flat_shape), back_state)
    shape = queries.shape
    return (
        attended.reshape(shape),
        grad_query.reshape(shape),
        grad_key.reshape(shape),
        grad_value.reshape(shape),
    )


def solution(mesh):
    placed = (
        P("orbit", "space", None, None),
        P("orbit", "space", None, None),
        P("orbit", "space", None, None),
        P(),
        P("orbit", "space", None, None),
    )
    return jax.shard_map(
        on_device_body,
        mesh=mesh,
        in_specs=placed,
        out_specs=(
            P("orbit", "space", None, None),
            P("orbit", "space", None, None),
            P("orbit", "space", None, None),
            P("orbit", "space", None, None),
        ),
        check_vma=False,
    )
```

```python
import jax
import jax.numpy as jnp
from jax import lax
from jax.experimental import pallas as pl
from jax.sharding import PartitionSpec as P

HEADS = 20
HD = 112


def padded_pair(cells, width):
    count = lax.axis_size("space")
    ends = count - 1
    rows = cells.shape[2]
    head = cells[:, :, :width]
    tail = cells[:, :, rows - width :]
    above = lax.ppermute(tail, "space", [(i, (i + 1) % count) for i in range(ends)])
    below = lax.ppermute(head, "space", [((i + 1) % count, i) for i in range(ends)])
    return jnp.concatenate([above, cells, below], axis=2)


ROWS = HEADS * HD
PACKED = 2304
LANES = 128
NORM = HD


def lane_one(tokens):
    lanes = lax.broadcasted_iota(jnp.int32, (tokens, LANES - HD), 1)
    return (lanes == 0).astype(jnp.bfloat16)


def part_kernel(k_ref, v_ref, s_ref):
    s_ref[ROWS:, :] = jnp.zeros((PACKED - ROWS, LANES), jnp.float32)
    extra = lane_one(k_ref.shape[0])
    for h in range(HEADS):
        cols = slice(h * HD, (h + 1) * HD)
        kf = jnp.maximum(k_ref[:, cols], 0)
        v_ext = jnp.concatenate([v_ref[:, cols], extra], axis=1)
        s_ref[h * HD : (h + 1) * HD, :] = lax.dot_general(
            kf, v_ext, (((0,), (0,)), ((), ())), preferred_element_type=jnp.float32
        )


def tile_kernel(q_ref, g_ref, k_ref, v_ref, qt_ref, qx_ref, gt_ref, kt_ref, vt_ref):
    tokens = q_ref.shape[0]
    zero = jnp.zeros((tokens, LANES - HD), jnp.bfloat16)
    extra = lane_one(tokens)
    for h in range(HEADS):
        cols = slice(h * HD, (h + 1) * HD)
        qf = jnp.concatenate([jnp.maximum(q_ref[:, cols], 0), zero], axis=1)
        qt_ref[h] = qf
        qx_ref[h] = qf.T
        gt_ref[h] = jnp.concatenate([g_ref[:, cols], zero], axis=1)
        kt_ref[h] = jnp.concatenate([jnp.maximum(k_ref[:, cols], 0), zero], axis=1)
        vt_ref[h] = jnp.concatenate([v_ref[:, cols], extra], axis=1)


def state_grad_kernel(qt_ref, qx_ref, gt_ref, s_ref, sg_ref):
    sg_ref[ROWS:, :] = jnp.zeros((PACKED - ROWS, LANES), jnp.float32)
    lanes = lax.broadcasted_iota(jnp.int32, (qt_ref.shape[1], LANES), 1)
    for h in range(HEADS):
        state = s_ref[h * HD : h * HD + LANES, :]
        wide = jnp.dot(qt_ref[h], state, preferred_element_type=jnp.float32)
        denominator = wide[:, NORM : NORM + 1] + 1.0
        inverse = 1.0 / denominator
        gw = gt_ref[h].astype(jnp.float32)
        num_grad = (gw * inverse).astype(jnp.bfloat16)
        den_grad = (
            -jnp.sum(gw * wide, axis=1, keepdims=True) / (denominator * denominator)
        ).astype(jnp.bfloat16)
        grads = jnp.where(lanes == NORM, den_grad, num_grad)
        sg = jnp.dot(qx_ref[h], grads, preferred_element_type=jnp.float32)
        sg_ref[h * HD : (h + 1) * HD, :] = sg[:HD]


def forward_kernel(qt_ref, gt_ref, c_ref, s_ref, a_ref, gq_ref):
    lanes = lax.broadcasted_iota(jnp.int32, (qt_ref.shape[1], LANES), 1)
    for h in range(HEADS):
        cols = slice(h * HD, (h + 1) * HD)
        qf = qt_ref[h]
        wide = jnp.dot(qf, s_ref[h * HD : h * HD + LANES, :], preferred_element_type=jnp.float32)
        denominator = wide[:, NORM : NORM + 1] + 1.0
        inverse = 1.0 / denominator
        a_ref[:, cols] = (wide[:, :HD] * inverse + c_ref[:, cols]).astype(jnp.bfloat16)
        gw = gt_ref[h].astype(jnp.float32)
        num_grad = (gw * inverse).astype(jnp.bfloat16)
        den_grad = (
            -jnp.sum(gw * wide, axis=1, keepdims=True) / (denominator * denominator)
        ).astype(jnp.bfloat16)
        grads = jnp.where(lanes == NORM, den_grad, num_grad)
        query_grad = lax.dot_general(
            grads, s_ref[h * HD : (h + 1) * HD, :], (((1,), (1,)), ((), ())),
            preferred_element_type=jnp.float32,
        )
        gq_ref[:, cols] = jnp.where(qf[:, :HD] > 0, query_grad, 0.0).astype(jnp.bfloat16)


def backward_kernel(kt_ref, vt_ref, c_ref, s_ref, gk_ref, gv_ref):
    for h in range(HEADS):
        cols = slice(h * HD, (h + 1) * HD)
        kf = kt_ref[h]
        key_grad = lax.dot_general(
            vt_ref[h], s_ref[h * HD : (h + 1) * HD, :], (((1,), (1,)), ((), ())),
            preferred_element_type=jnp.float32,
        )
        gk_ref[:, cols] = jnp.where(kf[:, :HD] > 0, key_grad, 0.0).astype(jnp.bfloat16)
        state = s_ref[h * HD : h * HD + LANES, :]
        value_grad = jnp.dot(kf, state, preferred_element_type=jnp.float32)[:, :HD]
        gv_ref[:, cols] = (value_grad + c_ref[:, cols]).astype(jnp.bfloat16)


def spread_states(packed, reverse, counts):
    space = lax.axis_size("space")
    orbit = lax.axis_size("orbit")
    place = lax.axis_index("orbit")
    pieces = lax.all_to_all(packed.reshape(space, -1, LANES), "space", 0, 0, tiled=True)
    whole = jnp.sum(pieces, axis=0)[:, : NORM + 1]
    views = jnp.arange(orbit)
    if not reverse:
        gathered = lax.all_gather(whole, "orbit")
        keep = views <= place
        summed = jnp.sum(jnp.where(keep[:, None, None], gathered, 0.0), axis=0)
        summed = summed / counts
    else:
        whole = whole / counts
        gathered = lax.all_gather(whole, "orbit")
        keep = views >= place
        summed = jnp.sum(jnp.where(keep[:, None, None], gathered, 0.0), axis=0)
    rounded = jnp.pad(summed.astype(jnp.bfloat16), ((0, 0), (0, LANES - NORM - 1)))
    return lax.all_gather(rounded, "space", tiled=True)


def on_device_body(queries, keys_in, values, conv_weight, grad_out):
    view_count, row_count, col_count, feature_width = queries.shape
    token_count = view_count * row_count * col_count
    flat_shape = (token_count, feature_width)
    q2 = queries.reshape(flat_shape)
    k2 = keys_in.reshape(flat_shape)
    v2 = values.reshape(flat_shape)
    g2 = grad_out.reshape(flat_shape)
    place = lax.axis_index("orbit")
    count = (place.astype(jnp.float32) + 1.0) * float(
        row_count * lax.axis_size("space") * col_count
    )
    f32 = jnp.float32
    packed_part = pl.pallas_call(
        part_kernel, out_shape=jax.ShapeDtypeStruct((PACKED, LANES), f32)
    )(k2, v2)
    tile = jax.ShapeDtypeStruct((HEADS, token_count, LANES), jnp.bfloat16)
    q_tiles, q_cross, g_tiles, k_tiles, v_tiles = pl.pallas_call(
        tile_kernel, out_shape=(tile,) * 5
    )(q2, g2, k2, v2)
    state_b = spread_states(packed_part, False, count)

    pair = padded_pair(jnp.stack([values, grad_out]), 1)
    pair = jnp.pad(pair, ((0, 0), (0, 0), (0, 0), (1, 1), (0, 0)))
    value_pad, grad_pad = pair[0], pair[1]
    weight_wide = conv_weight.astype(f32)
    conv_term = jnp.zeros(queries.shape, f32)
    conv_grad = jnp.zeros(queries.shape, f32)
    for row_step in range(3):
        for col_step in range(3):
            conv_term = conv_term + weight_wide[row_step, col_step] * value_pad[
                :, row_step : row_step + row_count, col_step : col_step + col_count
            ].astype(f32)
            conv_grad = conv_grad + weight_wide[row_step, col_step] * grad_pad[
                :, 2 - row_step : 2 - row_step + row_count, 2 - col_step : 2 - col_step + col_count
            ].astype(f32)

    bf = jnp.bfloat16
    state_grad = pl.pallas_call(
        state_grad_kernel, out_shape=jax.ShapeDtypeStruct((PACKED, LANES), f32)
    )(q_tiles, q_cross, g_tiles, state_b)
    conv_flat = conv_term.reshape(flat_shape)
    attended, grad_query = pl.pallas_call(
        forward_kernel,
        out_shape=(
            jax.ShapeDtypeStruct(flat_shape, bf),
            jax.ShapeDtypeStruct(flat_shape, bf),
        ),
    )(q_tiles, g_tiles, conv_flat, state_b)
    back_state = spread_states(state_grad, True, count)
    grad_key, grad_value = pl.pallas_call(
        backward_kernel,
        out_shape=(
            jax.ShapeDtypeStruct(flat_shape, bf),
            jax.ShapeDtypeStruct(flat_shape, bf),
        ),
    )(k_tiles, v_tiles, conv_grad.reshape(flat_shape), back_state)
    shape = queries.shape
    return (
        attended.reshape(shape),
        grad_query.reshape(shape),
        grad_key.reshape(shape),
        grad_value.reshape(shape),
    )


def solution(mesh):
    placed = (
        P("orbit", "space", None, None),
        P("orbit", "space", None, None),
        P("orbit", "space", None, None),
        P(),
        P("orbit", "space", None, None),
    )
    return jax.shard_map(
        on_device_body,
        mesh=mesh,
        in_specs=placed,
        out_specs=(
            P("orbit", "space", None, None),
            P("orbit", "space", None, None),
            P("orbit", "space", None, None),
            P("orbit", "space", None, None),
        ),
        check_vma=False,
    )
```

```python
import jax
import jax.numpy as jnp
from jax import lax
from jax.experimental import pallas as pl
from jax.sharding import PartitionSpec as P

HEADS = 20
HD = 112


def padded_pair(cells, width):
    count = lax.axis_size("space")
    ends = count - 1
    rows = cells.shape[2]
    head = cells[:, :, :width]
    tail = cells[:, :, rows - width :]
    above = lax.ppermute(tail, "space", [(i, (i + 1) % count) for i in range(ends)])
    below = lax.ppermute(head, "space", [((i + 1) % count, i) for i in range(ends)])
    return jnp.concatenate([above, cells, below], axis=2)


ROWS = HEADS * HD
PACKED = 2304
LANES = 128
NORM = HD


def lane_one(tokens):
    lanes = lax.broadcasted_iota(jnp.int32, (tokens, LANES - HD), 1)
    return (lanes == 0).astype(jnp.bfloat16)


def part_kernel(k_ref, v_ref, s_ref):
    s_ref[ROWS:, :] = jnp.zeros((PACKED - ROWS, LANES), jnp.float32)
    extra = lane_one(k_ref.shape[0])
    for h in range(HEADS):
        cols = slice(h * HD, (h + 1) * HD)
        kf = jnp.maximum(k_ref[:, cols], 0)
        v_ext = jnp.concatenate([v_ref[:, cols], extra], axis=1)
        s_ref[h * HD : (h + 1) * HD, :] = lax.dot_general(
            kf, v_ext, (((0,), (0,)), ((), ())), preferred_element_type=jnp.float32
        )


def tile_kernel(q_ref, g_ref, k_ref, v_ref, qt_ref, qx_ref, gt_ref, kt_ref, vt_ref):
    tokens = q_ref.shape[0]
    zero = jnp.zeros((tokens, LANES - HD), jnp.bfloat16)
    extra = lane_one(tokens)
    for h in range(HEADS):
        cols = slice(h * HD, (h + 1) * HD)
        qf = jnp.concatenate([jnp.maximum(q_ref[:, cols], 0), zero], axis=1)
        qt_ref[h] = qf
        qx_ref[h] = qf.T
        gt_ref[h] = jnp.concatenate([g_ref[:, cols], zero], axis=1)
        kt_ref[h] = jnp.concatenate([jnp.maximum(k_ref[:, cols], 0), zero], axis=1)
        vt_ref[h] = jnp.concatenate([v_ref[:, cols], extra], axis=1)


def state_grad_kernel(qt_ref, qx_ref, gt_ref, s_ref, sg_ref):
    sg_ref[ROWS:, :] = jnp.zeros((PACKED - ROWS, LANES), jnp.float32)
    lanes = lax.broadcasted_iota(jnp.int32, (qt_ref.shape[1], LANES), 1)
    for h in range(HEADS):
        state = s_ref[h * HD : h * HD + LANES, :]
        wide = jnp.dot(qt_ref[h], state, preferred_element_type=jnp.float32)
        denominator = wide[:, NORM : NORM + 1] + 1.0
        inverse = 1.0 / denominator
        gw = gt_ref[h].astype(jnp.float32)
        num_grad = (gw * inverse).astype(jnp.bfloat16)
        den_grad = (
            -jnp.sum(gw * wide, axis=1, keepdims=True) / (denominator * denominator)
        ).astype(jnp.bfloat16)
        grads = jnp.where(lanes == NORM, den_grad, num_grad)
        sg = jnp.dot(qx_ref[h], grads, preferred_element_type=jnp.float32)
        sg_ref[h * HD : (h + 1) * HD, :] = sg[:HD]


def forward_kernel(qt_ref, gt_ref, c_ref, s_ref, a_ref, gq_ref):
    lanes = lax.broadcasted_iota(jnp.int32, (qt_ref.shape[1], LANES), 1)
    for h in range(HEADS):
        cols = slice(h * HD, (h + 1) * HD)
        qf = qt_ref[h]
        wide = jnp.dot(qf, s_ref[h * HD : h * HD + LANES, :], preferred_element_type=jnp.float32)
        denominator = wide[:, NORM : NORM + 1] + 1.0
        inverse = 1.0 / denominator
        a_ref[:, cols] = (wide[:, :HD] * inverse + c_ref[:, cols]).astype(jnp.bfloat16)
        gw = gt_ref[h].astype(jnp.float32)
        num_grad = (gw * inverse).astype(jnp.bfloat16)
        den_grad = (
            -jnp.sum(gw * wide, axis=1, keepdims=True) / (denominator * denominator)
        ).astype(jnp.bfloat16)
        grads = jnp.where(lanes == NORM, den_grad, num_grad)
        query_grad = lax.dot_general(
            grads, s_ref[h * HD : (h + 1) * HD, :], (((1,), (1,)), ((), ())),
            preferred_element_type=jnp.float32,
        )
        gq_ref[:, cols] = jnp.where(qf[:, :HD] > 0, query_grad, 0.0).astype(jnp.bfloat16)


def backward_kernel(kt_ref, vt_ref, c_ref, s_ref, gk_ref, gv_ref):
    for h in range(HEADS):
        cols = slice(h * HD, (h + 1) * HD)
        kf = kt_ref[h]
        key_grad = lax.dot_general(
            vt_ref[h], s_ref[h * HD : (h + 1) * HD, :], (((1,), (1,)), ((), ())),
            preferred_element_type=jnp.float32,
        )
        gk_ref[:, cols] = jnp.where(kf[:, :HD] > 0, key_grad, 0.0).astype(jnp.bfloat16)
        state = s_ref[h * HD : h * HD + LANES, :]
        value_grad = jnp.dot(kf, state, preferred_element_type=jnp.float32)[:, :HD]
        gv_ref[:, cols] = (value_grad + c_ref[:, cols]).astype(jnp.bfloat16)


def spread_states(packed, reverse, counts):
    space = lax.axis_size("space")
    orbit = lax.axis_size("orbit")
    place = lax.axis_index("orbit")
    pieces = lax.all_to_all(
        packed.astype(jnp.bfloat16).reshape(space, -1, LANES), "space", 0, 0, tiled=True
    )
    whole = jnp.sum(pieces.astype(jnp.float32), axis=0)[:, : NORM + 1]
    views = jnp.arange(orbit)
    if not reverse:
        gathered = lax.all_gather(whole, "orbit")
        keep = views <= place
        summed = jnp.sum(jnp.where(keep[:, None, None], gathered, 0.0), axis=0)
        summed = summed / counts
    else:
        whole = whole / counts
        gathered = lax.all_gather(whole, "orbit")
        keep = views >= place
        summed = jnp.sum(jnp.where(keep[:, None, None], gathered, 0.0), axis=0)
    rounded = jnp.pad(summed.astype(jnp.bfloat16), ((0, 0), (0, LANES - NORM - 1)))
    return lax.all_gather(rounded, "space", tiled=True)


def on_device_body(queries, keys_in, values, conv_weight, grad_out):
    view_count, row_count, col_count, feature_width = queries.shape
    token_count = view_count * row_count * col_count
    flat_shape = (token_count, feature_width)
    q2 = queries.reshape(flat_shape)
    k2 = keys_in.reshape(flat_shape)
    v2 = values.reshape(flat_shape)
    g2 = grad_out.reshape(flat_shape)
    place = lax.axis_index("orbit")
    count = (place.astype(jnp.float32) + 1.0) * float(
        row_count * lax.axis_size("space") * col_count
    )
    f32 = jnp.float32
    packed_part = pl.pallas_call(
        part_kernel, out_shape=jax.ShapeDtypeStruct((PACKED, LANES), f32)
    )(k2, v2)
    tile = jax.ShapeDtypeStruct((HEADS, token_count, LANES), jnp.bfloat16)
    q_tiles, q_cross, g_tiles, k_tiles, v_tiles = pl.pallas_call(
        tile_kernel, out_shape=(tile,) * 5
    )(q2, g2, k2, v2)
    state_b = spread_states(packed_part, False, count)

    pair = padded_pair(jnp.stack([values, grad_out]), 1)
    pair = jnp.pad(pair, ((0, 0), (0, 0), (0, 0), (1, 1), (0, 0)))
    value_pad, grad_pad = pair[0], pair[1]
    weight_wide = conv_weight.astype(f32)
    conv_term = jnp.zeros(queries.shape, f32)
    conv_grad = jnp.zeros(queries.shape, f32)
    for row_step in range(3):
        for col_step in range(3):
            conv_term = conv_term + weight_wide[row_step, col_step] * value_pad[
                :, row_step : row_step + row_count, col_step : col_step + col_count
            ].astype(f32)
            conv_grad = conv_grad + weight_wide[row_step, col_step] * grad_pad[
                :, 2 - row_step : 2 - row_step + row_count, 2 - col_step : 2 - col_step + col_count
            ].astype(f32)

    bf = jnp.bfloat16
    state_grad = pl.pallas_call(
        state_grad_kernel, out_shape=jax.ShapeDtypeStruct((PACKED, LANES), f32)
    )(q_tiles, q_cross, g_tiles, state_b)
    conv_flat = conv_term.reshape(flat_shape)
    attended, grad_query = pl.pallas_call(
        forward_kernel,
        out_shape=(
            jax.ShapeDtypeStruct(flat_shape, bf),
            jax.ShapeDtypeStruct(flat_shape, bf),
        ),
    )(q_tiles, g_tiles, conv_flat, state_b)
    back_state = spread_states(state_grad, True, count)
    grad_key, grad_value = pl.pallas_call(
        backward_kernel,
        out_shape=(
            jax.ShapeDtypeStruct(flat_shape, bf),
            jax.ShapeDtypeStruct(flat_shape, bf),
        ),
    )(k_tiles, v_tiles, conv_grad.reshape(flat_shape), back_state)
    shape = queries.shape
    return (
        attended.reshape(shape),
        grad_query.reshape(shape),
        grad_key.reshape(shape),
        grad_value.reshape(shape),
    )


def solution(mesh):
    placed = (
        P("orbit", "space", None, None),
        P("orbit", "space", None, None),
        P("orbit", "space", None, None),
        P(),
        P("orbit", "space", None, None),
    )
    return jax.shard_map(
        on_device_body,
        mesh=mesh,
        in_specs=placed,
        out_specs=(
            P("orbit", "space", None, None),
            P("orbit", "space", None, None),
            P("orbit", "space", None, None),
            P("orbit", "space", None, None),
        ),
        check_vma=False,
    )
```

```python
import jax
import jax.numpy as jnp
from jax import lax
from jax.experimental import pallas as pl
from jax.sharding import PartitionSpec as P

HEADS = 20
HD = 112


def halo_rows(cells, width):
    count = lax.axis_size("space")
    ends = count - 1
    rows = cells.shape[2]
    head = cells[:, :, :width]
    tail = cells[:, :, rows - width :]
    above = lax.ppermute(tail, "space", [(i, (i + 1) % count) for i in range(ends)])
    below = lax.ppermute(head, "space", [((i + 1) % count, i) for i in range(ends)])
    return above, below


ROWS = HEADS * HD
PACKED = 2304
LANES = 128
NORM = HD
WIDTH = NORM + 1


def lane_one(tokens):
    lanes = lax.broadcasted_iota(jnp.int32, (tokens, LANES - HD), 1)
    return (lanes == 0).astype(jnp.bfloat16)


def part_kernel(k_ref, v_ref, s_ref):
    s_ref[ROWS:, :] = jnp.zeros((PACKED - ROWS, WIDTH), jnp.float32)
    extra = jnp.ones((k_ref.shape[0], 1), jnp.bfloat16)
    for h in range(HEADS):
        cols = slice(h * HD, (h + 1) * HD)
        kf = jnp.maximum(k_ref[:, cols], 0)
        v_ext = jnp.concatenate([v_ref[:, cols], extra], axis=1)
        s_ref[h * HD : (h + 1) * HD, :] = lax.dot_general(
            kf, v_ext, (((0,), (0,)), ((), ())), preferred_element_type=jnp.float32
        )


def tile_kernel(q_ref, g_ref, k_ref, v_ref, qt_ref, qx_ref, gt_ref, kt_ref, vt_ref):
    tokens = q_ref.shape[0]
    zero = jnp.zeros((tokens, LANES - HD), jnp.bfloat16)
    extra = lane_one(tokens)
    for h in range(HEADS):
        cols = slice(h * HD, (h + 1) * HD)
        qf = jnp.concatenate([jnp.maximum(q_ref[:, cols], 0), zero], axis=1)
        qt_ref[h] = qf
        qx_ref[h] = qf.T
        gt_ref[h] = jnp.concatenate([g_ref[:, cols], zero], axis=1)
        kt_ref[h] = jnp.concatenate([jnp.maximum(k_ref[:, cols], 0), zero], axis=1)
        vt_ref[h] = jnp.concatenate([v_ref[:, cols], extra], axis=1)


def state_grad_kernel(qt_ref, qx_ref, gt_ref, s_ref, sg_ref):
    sg_ref[ROWS:, :] = jnp.zeros((PACKED - ROWS, WIDTH), jnp.float32)
    lanes = lax.broadcasted_iota(jnp.int32, (qt_ref.shape[1], WIDTH), 1)
    for h in range(HEADS):
        state = s_ref[h * HD : h * HD + LANES, :]
        wide = jnp.dot(qt_ref[h], state, preferred_element_type=jnp.float32)
        denominator = wide[:, NORM : NORM + 1] + 1.0
        inverse = 1.0 / denominator
        gw = gt_ref[h][:, :WIDTH].astype(jnp.float32)
        num_grad = (gw * inverse).astype(jnp.bfloat16)
        den_grad = (
            -jnp.sum(gw * wide, axis=1, keepdims=True) / (denominator * denominator)
        ).astype(jnp.bfloat16)
        grads = jnp.where(lanes == NORM, den_grad, num_grad)
        sg = jnp.dot(qx_ref[h], grads, preferred_element_type=jnp.float32)
        sg_ref[h * HD : (h + 1) * HD, :] = sg[:HD]


def forward_kernel(qt_ref, gt_ref, c_ref, s_ref, a_ref, gq_ref):
    lanes = lax.broadcasted_iota(jnp.int32, (qt_ref.shape[1], WIDTH), 1)
    for h in range(HEADS):
        cols = slice(h * HD, (h + 1) * HD)
        qf = qt_ref[h]
        wide = jnp.dot(qf, s_ref[h * HD : h * HD + LANES, :], preferred_element_type=jnp.float32)
        denominator = wide[:, NORM : NORM + 1] + 1.0
        inverse = 1.0 / denominator
        a_ref[:, cols] = (wide[:, :HD] * inverse + c_ref[:, cols]).astype(jnp.bfloat16)
        gw = gt_ref[h][:, :WIDTH].astype(jnp.float32)
        num_grad = (gw * inverse).astype(jnp.bfloat16)
        den_grad = (
            -jnp.sum(gw * wide, axis=1, keepdims=True) / (denominator * denominator)
        ).astype(jnp.bfloat16)
        grads = jnp.where(lanes == NORM, den_grad, num_grad)
        query_grad = lax.dot_general(
            grads, s_ref[h * HD : (h + 1) * HD, :], (((1,), (1,)), ((), ())),
            preferred_element_type=jnp.float32,
        )
        gq_ref[:, cols] = jnp.where(qf[:, :HD] > 0, query_grad, 0.0).astype(jnp.bfloat16)


def backward_kernel(kt_ref, vt_ref, c_ref, s_ref, gk_ref, gv_ref):
    for h in range(HEADS):
        cols = slice(h * HD, (h + 1) * HD)
        kf = kt_ref[h]
        key_grad = lax.dot_general(
            vt_ref[h][:, :WIDTH], s_ref[h * HD : (h + 1) * HD, :], (((1,), (1,)), ((), ())),
            preferred_element_type=jnp.float32,
        )
        gk_ref[:, cols] = jnp.where(kf[:, :HD] > 0, key_grad, 0.0).astype(jnp.bfloat16)
        state = s_ref[h * HD : h * HD + LANES, :]
        value_grad = jnp.dot(kf, state, preferred_element_type=jnp.float32)[:, :HD]
        gv_ref[:, cols] = (value_grad + c_ref[:, cols]).astype(jnp.bfloat16)


def spread_states(packed, reverse, counts, tie=None):
    space = lax.axis_size("space")
    orbit = lax.axis_size("orbit")
    place = lax.axis_index("orbit")
    pieces = lax.all_to_all(packed.reshape(space, -1, WIDTH), "space", 0, 0, tiled=True)
    pieces, tie = lax.optimization_barrier((pieces, tie))
    whole = jnp.sum(pieces, axis=0)
    views = jnp.arange(orbit)
    if not reverse:
        gathered = lax.all_gather(whole, "orbit")
        keep = views <= place
        summed = jnp.sum(jnp.where(keep[:, None, None], gathered, 0.0), axis=0)
        summed = summed / counts
    else:
        whole = whole / counts
        gathered = lax.all_gather(whole, "orbit")
        keep = views >= place
        summed = jnp.sum(jnp.where(keep[:, None, None], gathered, 0.0), axis=0)
    return lax.all_gather(summed.astype(jnp.bfloat16), "space", tiled=True), tie


def on_device_body(queries, keys_in, values, conv_weight, grad_out):
    view_count, row_count, col_count, feature_width = queries.shape
    token_count = view_count * row_count * col_count
    flat_shape = (token_count, feature_width)
    q2 = queries.reshape(flat_shape)
    k2 = keys_in.reshape(flat_shape)
    v2 = values.reshape(flat_shape)
    g2 = grad_out.reshape(flat_shape)
    place = lax.axis_index("orbit")
    count = (place.astype(jnp.float32) + 1.0) * float(
        row_count * lax.axis_size("space") * col_count
    )
    f32 = jnp.float32
    packed_part = pl.pallas_call(
        part_kernel, out_shape=jax.ShapeDtypeStruct((PACKED, WIDTH), f32)
    )(k2, v2)
    tile = jax.ShapeDtypeStruct((HEADS, token_count, LANES), jnp.bfloat16)
    q_tiles, q_cross, g_tiles, k_tiles, v_tiles = pl.pallas_call(
        tile_kernel, out_shape=(tile,) * 5
    )(q2, g2, k2, v2)
    cells = jnp.stack([values, grad_out])
    halo = halo_rows(cells, 1)
    state_b, (above, below) = spread_states(packed_part, False, count, halo)

    pair = jnp.concatenate([above, cells, below], axis=2)
    pair = jnp.pad(pair, ((0, 0), (0, 0), (0, 0), (1, 1), (0, 0)))
    value_pad, grad_pad = pair[0], pair[1]
    weight_wide = conv_weight.astype(f32)
    conv_term = jnp.zeros(queries.shape, f32)
    conv_grad = jnp.zeros(queries.shape, f32)
    for row_step in range(3):
        for col_step in range(3):
            conv_term = conv_term + weight_wide[row_step, col_step] * value_pad[
                :, row_step : row_step + row_count, col_step : col_step + col_count
            ].astype(f32)
            conv_grad = conv_grad + weight_wide[row_step, col_step] * grad_pad[
                :, 2 - row_step : 2 - row_step + row_count, 2 - col_step : 2 - col_step + col_count
            ].astype(f32)

    bf = jnp.bfloat16
    state_grad = pl.pallas_call(
        state_grad_kernel, out_shape=jax.ShapeDtypeStruct((PACKED, WIDTH), f32)
    )(q_tiles, q_cross, g_tiles, state_b)
    conv_flat = conv_term.reshape(flat_shape)
    attended, grad_query = pl.pallas_call(
        forward_kernel,
        out_shape=(
            jax.ShapeDtypeStruct(flat_shape, bf),
            jax.ShapeDtypeStruct(flat_shape, bf),
        ),
    )(q_tiles, g_tiles, conv_flat, state_b)
    back_state, _ = spread_states(state_grad, True, count)
    grad_key, grad_value = pl.pallas_call(
        backward_kernel,
        out_shape=(
            jax.ShapeDtypeStruct(flat_shape, bf),
            jax.ShapeDtypeStruct(flat_shape, bf),
        ),
    )(k_tiles, v_tiles, conv_grad.reshape(flat_shape), back_state)
    shape = queries.shape
    return (
        attended.reshape(shape),
        grad_query.reshape(shape),
        grad_key.reshape(shape),
        grad_value.reshape(shape),
    )


def solution(mesh):
    placed = (
        P("orbit", "space", None, None),
        P("orbit", "space", None, None),
        P("orbit", "space", None, None),
        P(),
        P("orbit", "space", None, None),
    )
    return jax.shard_map(
        on_device_body,
        mesh=mesh,
        in_specs=placed,
        out_specs=(
            P("orbit", "space", None, None),
            P("orbit", "space", None, None),
            P("orbit", "space", None, None),
            P("orbit", "space", None, None),
        ),
        check_vma=False,
    )
```

```python
import jax
import jax.numpy as jnp
from jax import lax
from jax.experimental import pallas as pl
from jax.sharding import PartitionSpec as P

HEADS = 20
HD = 112


def padded_pair(cells, width):
    count = lax.axis_size("space")
    ends = count - 1
    rows = cells.shape[2]
    head = cells[:, :, :width]
    tail = cells[:, :, rows - width :]
    above = lax.ppermute(tail, "space", [(i, (i + 1) % count) for i in range(ends)])
    below = lax.ppermute(head, "space", [((i + 1) % count, i) for i in range(ends)])
    return jnp.concatenate([above, cells, below], axis=2)


ROWS = HEADS * HD
PACKED = 2304
LANES = 128
NORM = HD
WIDTH = NORM + 1


def lane_one(tokens):
    lanes = lax.broadcasted_iota(jnp.int32, (tokens, LANES - HD), 1)
    return (lanes == 0).astype(jnp.bfloat16)


def part_kernel(k_ref, v_ref, s_ref):
    s_ref[ROWS:, :] = jnp.zeros((PACKED - ROWS, WIDTH), jnp.float32)
    extra = jnp.ones((k_ref.shape[0], 1), jnp.bfloat16)
    for h in range(HEADS):
        cols = slice(h * HD, (h + 1) * HD)
        kf = jnp.maximum(k_ref[:, cols], 0)
        v_ext = jnp.concatenate([v_ref[:, cols], extra], axis=1)
        s_ref[h * HD : (h + 1) * HD, :] = lax.dot_general(
            kf, v_ext, (((0,), (0,)), ((), ())), preferred_element_type=jnp.float32
        )


def tile_kernel(q_ref, g_ref, k_ref, v_ref, qt_ref, qx_ref, gt_ref, kt_ref, vt_ref):
    tokens = q_ref.shape[0]
    zero = jnp.zeros((tokens, LANES - HD), jnp.bfloat16)
    extra = lane_one(tokens)
    for h in range(HEADS):
        cols = slice(h * HD, (h + 1) * HD)
        qf = jnp.concatenate([jnp.maximum(q_ref[:, cols], 0), zero], axis=1)
        qt_ref[h] = qf
        qx_ref[h] = qf.T
        gt_ref[h] = jnp.concatenate([g_ref[:, cols], zero], axis=1)
        kt_ref[h] = jnp.concatenate([jnp.maximum(k_ref[:, cols], 0), zero], axis=1)
        vt_ref[h] = jnp.concatenate([v_ref[:, cols], extra], axis=1)


def state_grad_kernel(qt_ref, qx_ref, gt_ref, s_ref, sg_ref):
    sg_ref[ROWS:, :] = jnp.zeros((PACKED - ROWS, WIDTH), jnp.float32)
    lanes = lax.broadcasted_iota(jnp.int32, (qt_ref.shape[1], WIDTH), 1)
    for h in range(HEADS):
        state = s_ref[h * HD : h * HD + LANES, :]
        wide = jnp.dot(qt_ref[h], state, preferred_element_type=jnp.float32)
        denominator = wide[:, NORM : NORM + 1] + 1.0
        inverse = 1.0 / denominator
        gw = gt_ref[h][:, :WIDTH].astype(jnp.float32)
        num_grad = (gw * inverse).astype(jnp.bfloat16)
        den_grad = (
            -jnp.sum(gw * wide, axis=1, keepdims=True) / (denominator * denominator)
        ).astype(jnp.bfloat16)
        grads = jnp.where(lanes == NORM, den_grad, num_grad)
        sg = jnp.dot(qx_ref[h], grads, preferred_element_type=jnp.float32)
        sg_ref[h * HD : (h + 1) * HD, :] = sg[:HD]


def forward_kernel(qt_ref, gt_ref, c_ref, s_ref, a_ref, gq_ref):
    lanes = lax.broadcasted_iota(jnp.int32, (qt_ref.shape[1], WIDTH), 1)
    for h in range(HEADS):
        cols = slice(h * HD, (h + 1) * HD)
        qf = qt_ref[h]
        wide = jnp.dot(qf, s_ref[h * HD : h * HD + LANES, :], preferred_element_type=jnp.float32)
        denominator = wide[:, NORM : NORM + 1] + 1.0
        inverse = 1.0 / denominator
        a_ref[:, cols] = (wide[:, :HD] * inverse + c_ref[:, cols]).astype(jnp.bfloat16)
        gw = gt_ref[h][:, :WIDTH].astype(jnp.float32)
        num_grad = (gw * inverse).astype(jnp.bfloat16)
        den_grad = (
            -jnp.sum(gw * wide, axis=1, keepdims=True) / (denominator * denominator)
        ).astype(jnp.bfloat16)
        grads = jnp.where(lanes == NORM, den_grad, num_grad)
        query_grad = lax.dot_general(
            grads, s_ref[h * HD : (h + 1) * HD, :], (((1,), (1,)), ((), ())),
            preferred_element_type=jnp.float32,
        )
        gq_ref[:, cols] = jnp.where(qf[:, :HD] > 0, query_grad, 0.0).astype(jnp.bfloat16)


def backward_kernel(kt_ref, vt_ref, c_ref, s_ref, gk_ref, gv_ref):
    for h in range(HEADS):
        cols = slice(h * HD, (h + 1) * HD)
        kf = kt_ref[h]
        key_grad = lax.dot_general(
            vt_ref[h][:, :WIDTH], s_ref[h * HD : (h + 1) * HD, :], (((1,), (1,)), ((), ())),
            preferred_element_type=jnp.float32,
        )
        gk_ref[:, cols] = jnp.where(kf[:, :HD] > 0, key_grad, 0.0).astype(jnp.bfloat16)
        state = s_ref[h * HD : h * HD + LANES, :]
        value_grad = jnp.dot(kf, state, preferred_element_type=jnp.float32)[:, :HD]
        gv_ref[:, cols] = (value_grad + c_ref[:, cols]).astype(jnp.bfloat16)


def spread_states(packed, reverse, counts):
    space = lax.axis_size("space")
    orbit = lax.axis_size("orbit")
    place = lax.axis_index("orbit")
    pieces = lax.all_to_all(packed.reshape(space, -1, WIDTH), "space", 0, 0, tiled=True)
    whole = jnp.sum(pieces, axis=0)
    views = jnp.arange(orbit)
    if not reverse:
        gathered = lax.all_gather(whole, "orbit")
        keep = views <= place
        summed = jnp.sum(jnp.where(keep[:, None, None], gathered, 0.0), axis=0)
        summed = summed / counts
    else:
        whole = whole / counts
        gathered = lax.all_gather(whole, "orbit")
        keep = views >= place
        summed = jnp.sum(jnp.where(keep[:, None, None], gathered, 0.0), axis=0)
    return lax.all_gather(summed.astype(jnp.bfloat16), "space", tiled=True)


def on_device_body(queries, keys_in, values, conv_weight, grad_out):
    view_count, row_count, col_count, feature_width = queries.shape
    token_count = view_count * row_count * col_count
    flat_shape = (token_count, feature_width)
    q2 = queries.reshape(flat_shape)
    k2 = keys_in.reshape(flat_shape)
    v2 = values.reshape(flat_shape)
    g2 = grad_out.reshape(flat_shape)
    place = lax.axis_index("orbit")
    count = (place.astype(jnp.float32) + 1.0) * float(
        row_count * lax.axis_size("space") * col_count
    )
    f32 = jnp.float32
    packed_part = pl.pallas_call(
        part_kernel, out_shape=jax.ShapeDtypeStruct((PACKED, WIDTH), f32)
    )(k2, v2)
    tile = jax.ShapeDtypeStruct((HEADS, token_count, LANES), jnp.bfloat16)
    q_tiles, q_cross, g_tiles, k_tiles, v_tiles = pl.pallas_call(
        tile_kernel, out_shape=(tile,) * 5
    )(q2, g2, k2, v2)
    state_b = spread_states(packed_part, False, count)

    pair = padded_pair(jnp.stack([values, grad_out]), 1)
    pair = jnp.pad(pair, ((0, 0), (0, 0), (0, 0), (1, 1), (0, 0)))
    value_pad, grad_pad = pair[0], pair[1]
    weight_wide = conv_weight.astype(f32)
    conv_term = jnp.zeros(queries.shape, f32)
    conv_grad = jnp.zeros(queries.shape, f32)
    for row_step in range(3):
        for col_step in range(3):
            conv_term = conv_term + weight_wide[row_step, col_step] * value_pad[
                :, row_step : row_step + row_count, col_step : col_step + col_count
            ].astype(f32)
            conv_grad = conv_grad + weight_wide[row_step, col_step] * grad_pad[
                :, 2 - row_step : 2 - row_step + row_count, 2 - col_step : 2 - col_step + col_count
            ].astype(f32)

    bf = jnp.bfloat16
    state_grad = pl.pallas_call(
        state_grad_kernel, out_shape=jax.ShapeDtypeStruct((PACKED, WIDTH), f32)
    )(q_tiles, q_cross, g_tiles, state_b)
    conv_flat = conv_term.reshape(flat_shape)
    attended, grad_query = pl.pallas_call(
        forward_kernel,
        out_shape=(
            jax.ShapeDtypeStruct(flat_shape, bf),
            jax.ShapeDtypeStruct(flat_shape, bf),
        ),
    )(q_tiles, g_tiles, conv_flat, state_b)
    back_state = spread_states(state_grad, True, count)
    grad_key, grad_value = pl.pallas_call(
        backward_kernel,
        out_shape=(
            jax.ShapeDtypeStruct(flat_shape, bf),
            jax.ShapeDtypeStruct(flat_shape, bf),
        ),
    )(k_tiles, v_tiles, conv_grad.reshape(flat_shape), back_state)
    shape = queries.shape
    return (
        attended.reshape(shape),
        grad_query.reshape(shape),
        grad_key.reshape(shape),
        grad_value.reshape(shape),
    )


def solution(mesh):
    placed = (
        P("orbit", "space", None, None),
        P("orbit", "space", None, None),
        P("orbit", "space", None, None),
        P(),
        P("orbit", "space", None, None),
    )
    return jax.shard_map(
        on_device_body,
        mesh=mesh,
        in_specs=placed,
        out_specs=(
            P("orbit", "space", None, None),
            P("orbit", "space", None, None),
            P("orbit", "space", None, None),
            P("orbit", "space", None, None),
        ),
        check_vma=False,
    )
```

```python
import jax
import jax.numpy as jnp
from jax import lax
from jax.experimental import pallas as pl
from jax.sharding import PartitionSpec as P

HEADS = 20
HD = 112


def padded_pair(cells, width):
    count = lax.axis_size("space")
    ends = count - 1
    rows = cells.shape[2]
    head = cells[:, :, :width]
    tail = cells[:, :, rows - width :]
    above = lax.ppermute(tail, "space", [(i, (i + 1) % count) for i in range(ends)])
    below = lax.ppermute(head, "space", [((i + 1) % count, i) for i in range(ends)])
    return jnp.concatenate([above, cells, below], axis=2)


ROWS = HEADS * HD
PACKED = 2304
LANES = 128
NORM = HD
WIDTH = NORM + 1


def lane_one(tokens):
    lanes = lax.broadcasted_iota(jnp.int32, (tokens, LANES - HD), 1)
    return (lanes == 0).astype(jnp.bfloat16)


def part_kernel(k_ref, v_ref, s_ref):
    s_ref[ROWS:, :] = jnp.zeros((PACKED - ROWS, WIDTH), jnp.float32)
    extra = jnp.ones((k_ref.shape[0], 1), jnp.bfloat16)
    for h in range(HEADS):
        cols = slice(h * HD, (h + 1) * HD)
        kf = jnp.maximum(k_ref[:, cols], 0)
        v_ext = jnp.concatenate([v_ref[:, cols], extra], axis=1)
        s_ref[h * HD : (h + 1) * HD, :] = lax.dot_general(
            kf, v_ext, (((0,), (0,)), ((), ())), preferred_element_type=jnp.float32
        )


def tile_kernel(q_ref, g_ref, k_ref, v_ref, qt_ref, gt_ref, kt_ref, vt_ref):
    tokens = q_ref.shape[0]
    zero = jnp.zeros((tokens, LANES - HD), jnp.bfloat16)
    extra = lane_one(tokens)
    for h in range(HEADS):
        cols = slice(h * HD, (h + 1) * HD)
        qf = jnp.concatenate([jnp.maximum(q_ref[:, cols], 0), zero], axis=1)
        qt_ref[h] = qf
        gt_ref[h] = jnp.concatenate([g_ref[:, cols], zero], axis=1)
        kt_ref[h] = jnp.concatenate([jnp.maximum(k_ref[:, cols], 0), zero], axis=1)
        vt_ref[h] = jnp.concatenate([v_ref[:, cols], extra], axis=1)


def state_grad_kernel(qt_ref, gt_ref, s_ref, sg_ref):
    sg_ref[ROWS:, :] = jnp.zeros((PACKED - ROWS, WIDTH), jnp.float32)
    lanes = lax.broadcasted_iota(jnp.int32, (qt_ref.shape[1], WIDTH), 1)
    for h in range(HEADS):
        state = s_ref[h * HD : h * HD + LANES, :]
        wide = jnp.dot(qt_ref[h], state, preferred_element_type=jnp.float32)
        denominator = wide[:, NORM : NORM + 1] + 1.0
        inverse = 1.0 / denominator
        gw = gt_ref[h][:, :WIDTH].astype(jnp.float32)
        num_grad = (gw * inverse).astype(jnp.bfloat16)
        den_grad = (
            -jnp.sum(gw * wide, axis=1, keepdims=True) / (denominator * denominator)
        ).astype(jnp.bfloat16)
        grads = jnp.where(lanes == NORM, den_grad, num_grad)
        sg = lax.dot_general(
            qt_ref[h], grads, (((0,), (0,)), ((), ())), preferred_element_type=jnp.float32
        )
        sg_ref[h * HD : (h + 1) * HD, :] = sg[:HD]


def forward_kernel(qt_ref, gt_ref, c_ref, s_ref, a_ref, gq_ref):
    lanes = lax.broadcasted_iota(jnp.int32, (qt_ref.shape[1], WIDTH), 1)
    for h in range(HEADS):
        cols = slice(h * HD, (h + 1) * HD)
        qf = qt_ref[h]
        wide = jnp.dot(qf, s_ref[h * HD : h * HD + LANES, :], preferred_element_type=jnp.float32)
        denominator = wide[:, NORM : NORM + 1] + 1.0
        inverse = 1.0 / denominator
        a_ref[:, cols] = (wide[:, :HD] * inverse + c_ref[:, cols]).astype(jnp.bfloat16)
        gw = gt_ref[h][:, :WIDTH].astype(jnp.float32)
        num_grad = (gw * inverse).astype(jnp.bfloat16)
        den_grad = (
            -jnp.sum(gw * wide, axis=1, keepdims=True) / (denominator * denominator)
        ).astype(jnp.bfloat16)
        grads = jnp.where(lanes == NORM, den_grad, num_grad)
        query_grad = lax.dot_general(
            grads, s_ref[h * HD : (h + 1) * HD, :], (((1,), (1,)), ((), ())),
            preferred_element_type=jnp.float32,
        )
        gq_ref[:, cols] = jnp.where(qf[:, :HD] > 0, query_grad, 0.0).astype(jnp.bfloat16)


def backward_kernel(kt_ref, vt_ref, c_ref, s_ref, gk_ref, gv_ref):
    for h in range(HEADS):
        cols = slice(h * HD, (h + 1) * HD)
        kf = kt_ref[h]
        key_grad = lax.dot_general(
            vt_ref[h][:, :WIDTH], s_ref[h * HD : (h + 1) * HD, :], (((1,), (1,)), ((), ())),
            preferred_element_type=jnp.float32,
        )
        gk_ref[:, cols] = jnp.where(kf[:, :HD] > 0, key_grad, 0.0).astype(jnp.bfloat16)
        state = s_ref[h * HD : h * HD + LANES, :]
        value_grad = jnp.dot(kf, state, preferred_element_type=jnp.float32)[:, :HD]
        gv_ref[:, cols] = (value_grad + c_ref[:, cols]).astype(jnp.bfloat16)


def spread_states(packed, reverse, counts):
    space = lax.axis_size("space")
    orbit = lax.axis_size("orbit")
    place = lax.axis_index("orbit")
    pieces = lax.all_to_all(packed.reshape(space, -1, WIDTH), "space", 0, 0, tiled=True)
    whole = jnp.sum(pieces, axis=0)
    views = jnp.arange(orbit)
    if not reverse:
        gathered = lax.all_gather(whole, "orbit")
        keep = views <= place
        summed = jnp.sum(jnp.where(keep[:, None, None], gathered, 0.0), axis=0)
        summed = summed / counts
    else:
        whole = whole / counts
        gathered = lax.all_gather(whole, "orbit")
        keep = views >= place
        summed = jnp.sum(jnp.where(keep[:, None, None], gathered, 0.0), axis=0)
    return lax.all_gather(summed.astype(jnp.bfloat16), "space", tiled=True)


def on_device_body(queries, keys_in, values, conv_weight, grad_out):
    view_count, row_count, col_count, feature_width = queries.shape
    token_count = view_count * row_count * col_count
    flat_shape = (token_count, feature_width)
    q2 = queries.reshape(flat_shape)
    k2 = keys_in.reshape(flat_shape)
    v2 = values.reshape(flat_shape)
    g2 = grad_out.reshape(flat_shape)
    place = lax.axis_index("orbit")
    count = (place.astype(jnp.float32) + 1.0) * float(
        row_count * lax.axis_size("space") * col_count
    )
    f32 = jnp.float32
    packed_part = pl.pallas_call(
        part_kernel, out_shape=jax.ShapeDtypeStruct((PACKED, WIDTH), f32)
    )(k2, v2)
    tile = jax.ShapeDtypeStruct((HEADS, token_count, LANES), jnp.bfloat16)
    q_tiles, g_tiles, k_tiles, v_tiles = pl.pallas_call(
        tile_kernel, out_shape=(tile,) * 4
    )(q2, g2, k2, v2)
    state_b = spread_states(packed_part, False, count)

    pair = padded_pair(jnp.stack([values, grad_out]), 1)
    pair = jnp.pad(pair, ((0, 0), (0, 0), (0, 0), (1, 1), (0, 0)))
    value_pad, grad_pad = pair[0], pair[1]
    weight_wide = conv_weight.astype(f32)
    conv_term = jnp.zeros(queries.shape, f32)
    conv_grad = jnp.zeros(queries.shape, f32)
    for row_step in range(3):
        for col_step in range(3):
            conv_term = conv_term + weight_wide[row_step, col_step] * value_pad[
                :, row_step : row_step + row_count, col_step : col_step + col_count
            ].astype(f32)
            conv_grad = conv_grad + weight_wide[row_step, col_step] * grad_pad[
                :, 2 - row_step : 2 - row_step + row_count, 2 - col_step : 2 - col_step + col_count
            ].astype(f32)

    bf = jnp.bfloat16
    state_grad = pl.pallas_call(
        state_grad_kernel, out_shape=jax.ShapeDtypeStruct((PACKED, WIDTH), f32)
    )(q_tiles, g_tiles, state_b)
    conv_flat = conv_term.reshape(flat_shape)
    attended, grad_query = pl.pallas_call(
        forward_kernel,
        out_shape=(
            jax.ShapeDtypeStruct(flat_shape, bf),
            jax.ShapeDtypeStruct(flat_shape, bf),
        ),
    )(q_tiles, g_tiles, conv_flat, state_b)
    back_state = spread_states(state_grad, True, count)
    grad_key, grad_value = pl.pallas_call(
        backward_kernel,
        out_shape=(
            jax.ShapeDtypeStruct(flat_shape, bf),
            jax.ShapeDtypeStruct(flat_shape, bf),
        ),
    )(k_tiles, v_tiles, conv_grad.reshape(flat_shape), back_state)
    shape = queries.shape
    return (
        attended.reshape(shape),
        grad_query.reshape(shape),
        grad_key.reshape(shape),
        grad_value.reshape(shape),
    )


def solution(mesh):
    placed = (
        P("orbit", "space", None, None),
        P("orbit", "space", None, None),
        P("orbit", "space", None, None),
        P(),
        P("orbit", "space", None, None),
    )
    return jax.shard_map(
        on_device_body,
        mesh=mesh,
        in_specs=placed,
        out_specs=(
            P("orbit", "space", None, None),
            P("orbit", "space", None, None),
            P("orbit", "space", None, None),
            P("orbit", "space", None, None),
        ),
        check_vma=False,
    )
```

```python
import jax
import jax.numpy as jnp
from jax import lax
from jax.experimental import pallas as pl
from jax.sharding import PartitionSpec as P

HEADS = 20
HD = 112


def padded_pair(cells, width):
    count = lax.axis_size("space")
    ends = count - 1
    rows = cells.shape[2]
    head = cells[:, :, :width]
    tail = cells[:, :, rows - width :]
    above = lax.ppermute(tail, "space", [(i, (i + 1) % count) for i in range(ends)])
    below = lax.ppermute(head, "space", [((i + 1) % count, i) for i in range(ends)])
    return jnp.concatenate([above, cells, below], axis=2)


ROWS = HEADS * HD
PACKED = 2304
LANES = 128
NORM = HD
WIDTH = NORM + 1


def lane_one(tokens):
    lanes = lax.broadcasted_iota(jnp.int32, (tokens, LANES - HD), 1)
    return (lanes == 0).astype(jnp.bfloat16)


def part_kernel(k_ref, v_ref, s_ref):
    s_ref[ROWS:, :] = jnp.zeros((PACKED - ROWS, WIDTH), jnp.float32)
    extra = jnp.ones((k_ref.shape[0], 1), jnp.bfloat16)
    for h in range(HEADS):
        cols = slice(h * HD, (h + 1) * HD)
        kf = jnp.maximum(k_ref[:, cols], 0)
        v_ext = jnp.concatenate([v_ref[:, cols], extra], axis=1)
        s_ref[h * HD : (h + 1) * HD, :] = lax.dot_general(
            kf, v_ext, (((0,), (0,)), ((), ())), preferred_element_type=jnp.float32
        )


def tile_kernel(q_ref, g_ref, k_ref, v_ref, qt_ref, gt_ref, kt_ref, vt_ref):
    tokens = q_ref.shape[0]
    zero = jnp.zeros((tokens, LANES - HD), jnp.bfloat16)
    extra = lane_one(tokens)
    for h in range(HEADS):
        cols = slice(h * HD, (h + 1) * HD)
        qf = jnp.concatenate([jnp.maximum(q_ref[:, cols], 0), zero], axis=1)
        qt_ref[h] = qf
        gt_ref[h] = jnp.concatenate([g_ref[:, cols], zero], axis=1)
        kt_ref[h] = jnp.concatenate([jnp.maximum(k_ref[:, cols], 0), zero], axis=1)
        vt_ref[h] = jnp.concatenate([v_ref[:, cols], extra], axis=1)


def state_grad_kernel(qt_ref, gt_ref, s_ref, sg_ref):
    sg_ref[ROWS:, :] = jnp.zeros((PACKED - ROWS, WIDTH), jnp.float32)
    lanes = lax.broadcasted_iota(jnp.int32, (qt_ref.shape[1], WIDTH), 1)
    for h in range(HEADS):
        state = s_ref[h * HD : h * HD + LANES, :]
        wide = jnp.dot(qt_ref[h], state, preferred_element_type=jnp.float32)
        denominator = wide[:, NORM : NORM + 1] + 1.0
        inverse = 1.0 / denominator
        gw = gt_ref[h][:, :WIDTH].astype(jnp.float32)
        num_grad = (gw * inverse).astype(jnp.bfloat16)
        den_grad = (
            -jnp.sum(gw * wide, axis=1, keepdims=True) / (denominator * denominator)
        ).astype(jnp.bfloat16)
        grads = jnp.where(lanes == NORM, den_grad, num_grad)
        sg = lax.dot_general(
            qt_ref[h], grads, (((0,), (0,)), ((), ())), preferred_element_type=jnp.float32
        )
        sg_ref[h * HD : (h + 1) * HD, :] = sg[:HD]


def forward_kernel(qt_ref, gt_ref, c_ref, s_ref, a_ref, gq_ref):
    lanes = lax.broadcasted_iota(jnp.int32, (qt_ref.shape[1], WIDTH), 1)
    for h in range(HEADS):
        cols = slice(h * HD, (h + 1) * HD)
        qf = qt_ref[h]
        wide = jnp.dot(qf, s_ref[h * HD : h * HD + LANES, :], preferred_element_type=jnp.float32)
        denominator = wide[:, NORM : NORM + 1] + 1.0
        inverse = 1.0 / denominator
        a_ref[:, cols] = (wide[:, :HD] * inverse + c_ref[:, cols]).astype(jnp.bfloat16)
        gw = gt_ref[h][:, :WIDTH].astype(jnp.float32)
        num_grad = (gw * inverse).astype(jnp.bfloat16)
        den_grad = (
            -jnp.sum(gw * wide, axis=1, keepdims=True) / (denominator * denominator)
        ).astype(jnp.bfloat16)
        grads = jnp.where(lanes == NORM, den_grad, num_grad)
        query_grad = lax.dot_general(
            grads, s_ref[h * HD : (h + 1) * HD, :], (((1,), (1,)), ((), ())),
            preferred_element_type=jnp.float32,
        )
        gq_ref[:, cols] = jnp.where(qf[:, :HD] > 0, query_grad, 0.0).astype(jnp.bfloat16)


def backward_kernel(kt_ref, vt_ref, c_ref, s_ref, gk_ref, gv_ref):
    for h in range(HEADS):
        cols = slice(h * HD, (h + 1) * HD)
        kf = kt_ref[h]
        key_grad = lax.dot_general(
            vt_ref[h][:, :WIDTH], s_ref[h * HD : (h + 1) * HD, :], (((1,), (1,)), ((), ())),
            preferred_element_type=jnp.float32,
        )
        gk_ref[:, cols] = jnp.where(kf[:, :HD] > 0, key_grad, 0.0).astype(jnp.bfloat16)
        state = s_ref[h * HD : h * HD + LANES, :]
        value_grad = jnp.dot(kf, state, preferred_element_type=jnp.float32) + c_ref[h]
        gv_ref[:, cols] = value_grad[:, :HD].astype(jnp.bfloat16)


def spread_states(packed, reverse, counts):
    space = lax.axis_size("space")
    orbit = lax.axis_size("orbit")
    place = lax.axis_index("orbit")
    pieces = lax.all_to_all(packed.reshape(space, -1, WIDTH), "space", 0, 0, tiled=True)
    whole = jnp.sum(pieces, axis=0)
    views = jnp.arange(orbit)
    if not reverse:
        gathered = lax.all_gather(whole, "orbit")
        keep = views <= place
        summed = jnp.sum(jnp.where(keep[:, None, None], gathered, 0.0), axis=0)
        summed = summed / counts
    else:
        whole = whole / counts
        gathered = lax.all_gather(whole, "orbit")
        keep = views >= place
        summed = jnp.sum(jnp.where(keep[:, None, None], gathered, 0.0), axis=0)
    return lax.all_gather(summed.astype(jnp.bfloat16), "space", tiled=True)


def on_device_body(queries, keys_in, values, conv_weight, grad_out):
    view_count, row_count, col_count, feature_width = queries.shape
    token_count = view_count * row_count * col_count
    flat_shape = (token_count, feature_width)
    q2 = queries.reshape(flat_shape)
    k2 = keys_in.reshape(flat_shape)
    v2 = values.reshape(flat_shape)
    g2 = grad_out.reshape(flat_shape)
    place = lax.axis_index("orbit")
    count = (place.astype(jnp.float32) + 1.0) * float(
        row_count * lax.axis_size("space") * col_count
    )
    f32 = jnp.float32
    packed_part = pl.pallas_call(
        part_kernel, out_shape=jax.ShapeDtypeStruct((PACKED, WIDTH), f32)
    )(k2, v2)
    tile = jax.ShapeDtypeStruct((HEADS, token_count, LANES), jnp.bfloat16)
    q_tiles, g_tiles, k_tiles, v_tiles = pl.pallas_call(
        tile_kernel, out_shape=(tile,) * 4
    )(q2, g2, k2, v2)
    state_b = spread_states(packed_part, False, count)

    pair = padded_pair(jnp.stack([values, grad_out]), 1)
    pair = jnp.pad(pair, ((0, 0), (0, 0), (0, 0), (1, 1), (0, 0)))
    value_pad, grad_pad = pair[0], pair[1]
    weight_wide = conv_weight.astype(f32)
    conv_term = jnp.zeros(queries.shape, f32)
    conv_grad = jnp.zeros(queries.shape, f32)
    for row_step in range(3):
        for col_step in range(3):
            conv_term = conv_term + weight_wide[row_step, col_step] * value_pad[
                :, row_step : row_step + row_count, col_step : col_step + col_count
            ].astype(f32)
            conv_grad = conv_grad + weight_wide[row_step, col_step] * grad_pad[
                :, 2 - row_step : 2 - row_step + row_count, 2 - col_step : 2 - col_step + col_count
            ].astype(f32)

    bf = jnp.bfloat16
    grad_tiles = jnp.pad(
        conv_grad.reshape(token_count, HEADS, HD), ((0, 0), (0, 0), (0, WIDTH - HD))
    ).transpose(1, 0, 2)
    state_grad = pl.pallas_call(
        state_grad_kernel, out_shape=jax.ShapeDtypeStruct((PACKED, WIDTH), f32)
    )(q_tiles, g_tiles, state_b)
    conv_flat = conv_term.reshape(flat_shape)
    attended, grad_query = pl.pallas_call(
        forward_kernel,
        out_shape=(
            jax.ShapeDtypeStruct(flat_shape, bf),
            jax.ShapeDtypeStruct(flat_shape, bf),
        ),
    )(q_tiles, g_tiles, conv_flat, state_b)
    back_state = spread_states(state_grad, True, count)
    grad_key, grad_value = pl.pallas_call(
        backward_kernel,
        out_shape=(
            jax.ShapeDtypeStruct(flat_shape, bf),
            jax.ShapeDtypeStruct(flat_shape, bf),
        ),
    )(k_tiles, v_tiles, grad_tiles, back_state)
    shape = queries.shape
    return (
        attended.reshape(shape),
        grad_query.reshape(shape),
        grad_key.reshape(shape),
        grad_value.reshape(shape),
    )


def solution(mesh):
    placed = (
        P("orbit", "space", None, None),
        P("orbit", "space", None, None),
        P("orbit", "space", None, None),
        P(),
        P("orbit", "space", None, None),
    )
    return jax.shard_map(
        on_device_body,
        mesh=mesh,
        in_specs=placed,
        out_specs=(
            P("orbit", "space", None, None),
            P("orbit", "space", None, None),
            P("orbit", "space", None, None),
            P("orbit", "space", None, None),
        ),
        check_vma=False,
    )
```
